32 devices in a mesh: groups: 2 (over y), pipe: 4 (over z), dp: 2 (over x), mp: 2 (over core).
Axes of the slice: x: 2, y: 2, z: 4, core: 2. Of those that a mesh axis runs over, the one named last changes fastest.
Arguments:
- latent: bfloat16 [4, 2, 2, 4, 16, 320], P(('groups', 'dp')), parts along dimension 0, may hold values from -6 to 6
- section_weight: bfloat16 [4, 2, 921600], P('pipe', None, 'mp'), may hold values from -0.01613743 to 0.01613743, as said below
- out_grad: bfloat16 [4, 2, 2, 4, 16, 320], P(('groups', 'dp')), parts along dimension 0, may hold values from -0.29882812 to 0.29882812
Outputs:
- section_grad: float32 [8, 921600], P(('groups', 'pipe'), 'mp'), parts along dimension 0
The draws below stay inside these ranges and needn't reach their ends.
There are 2 independent parts, one for each index of `groups`. The reference program is written for one: setup_inputs(seed, part) draws one part's arguments, and reference() takes and returns one part's arrays. A program takes and returns all parts, laid end to end along the dimension named above; an argument that names none is the same for every part. Nothing has to cross between parts.
Inputs may be any that keep to these rules, and one draw needn't show every extreme that they name: section_weight[j, 0] equals section_weight[3 - j, 0] and section_weight[j, 1] equals section_weight[3 - j, 1] for every j: both devices of a mirrored pair hold the same two blocks.
All inputs are finite; a program needn't handle non-finite values.
Results may differ from the reference program's by a relative error of at most 0.0065.
Values may be sent and summed in bfloat16 or wider, within the bound.
No kernel may reach another device: no remote copies, remote signals or barrier semaphores. Data moves between devices by JAX's collectives and lax.ppermute only.
A program may use at most 64 MiB of HBM per device.

```python
import jax
import jax.numpy as jnp
from jax import lax

C = 320
HGT = 4
WID = 16
MB = 2
SECTIONS = 4
HALF = 2
REPLICAS = 2


def draw_section_weight(key, part):
    limit = (12.0 * C) ** (-0.5)
    blocks = jax.random.uniform(key, (SECTIONS, 9 * C * C), jnp.float32, -limit, limit)
    rows = jnp.arange(SECTIONS, dtype=jnp.int32)
    lower = jnp.minimum(rows, SECTIONS - 1 - rows)
    upper = SECTIONS - 1 - lower
    return jnp.stack([blocks[lower], blocks[upper]], axis=1).astype(jnp.bfloat16)


def levels(rng, dims, pieces, smallest, largest):
    loudness, own = 1.0, jax.random.fold_in(rng, 6)
    for axis_at, parts in pieces:
        steps = jnp.exp(jax.random.uniform(jax.random.fold_in(own, axis_at), (parts,), jnp.float32, smallest / len(pieces), largest / len(pieces)))
        loudness = loudness * jnp.repeat(steps, dims[axis_at] // parts).reshape([-1 if axis == axis_at else 1 for axis in range(len(dims))])
    return loudness


def gaussian(key, shape, spread, reach, cuts=(), held_as=jnp.bfloat16):
    array = jax.random.normal(key, shape, jnp.float32) * spread
    if len(cuts) > 0:
        array = levels(key, shape, cuts, -0.22, 0.18) * array
    return jnp.clip(array, min=-reach, max=reach).astype(held_as)


def setup_inputs(seed: int = 0, part: int = 0) -> dict:
    key_of = jax.random.split(jax.random.key(seed), 4)
    part_keys = jax.random.split(jax.random.fold_in(key_of[3], part), 4)
    return {
        "latent": gaussian(part_keys[0], (REPLICAS, 2, MB, HGT, WID, C), 1.0, 6.0, ((0, 2),)),
        "section_weight": draw_section_weight(jax.random.fold_in(key_of[3], 71), part),
        "out_grad": gaussian(part_keys[2], (REPLICAS, 2, MB, HGT, WID, C), 0.05, 0.29882812, ((0, 2),)),
    }


def patches(image_in):
    img_rows, img_cols, channels = image_in.shape[-3], image_in.shape[-2], image_in.shape[-1]
    padded = jnp.pad(image_in, [(0, 0)] * (image_in.ndim - 3) + [(1, 1), (1, 1), (0, 0)])
    shifted = [padded[..., row_off:row_off + img_rows, col_off:col_off + img_cols, :] for row_off in range(3) for col_off in range(3)]
    return jnp.stack(shifted, axis=-2).reshape(-1, 9 * channels)


def silu_slope(pre_act):
    sigmoid = jax.nn.sigmoid(pre_act)
    return sigmoid * (1.0 + pre_act * (1.0 - sigmoid))


def kernel_of(section_weight, section_idx):
    which = 0 if section_idx < HALF else 1
    return section_weight[section_idx, which].reshape(C, 3, 3, C).transpose(1, 2, 3, 0)


def reference(latent, section_weight, out_grad):
    states = [latent.reshape(-1, HGT, WID, C)]
    pre_acts = []
    activations = []
    for section_idx in range(SECTIONS):
        current = states[-1]
        pre_act = current.astype(jnp.float32)
        if section_idx >= HALF:
            pre_act = pre_act + states[SECTIONS - section_idx].astype(jnp.float32)
        activation = jax.nn.silu(pre_act).astype(jnp.bfloat16)
        conv_out = jnp.dot(patches(activation), kernel_of(section_weight, section_idx).reshape(9 * C, C), preferred_element_type=jnp.float32)
        states.append((current.astype(jnp.float32) + conv_out.reshape(current.shape)).astype(jnp.bfloat16))
        pre_acts.append(pre_act)
        activations.append(activation)
    section_grads = []
    skip_terms = {}
    passed = out_grad.reshape(-1, HGT, WID, C)
    middle = jnp.zeros(passed.shape, jnp.float32)
    for section_idx in range(SECTIONS - 1, -1, -1):
        if section_idx >= HALF:
            cotangent = passed
        elif section_idx == HALF - 1:
            cotangent = (passed.astype(jnp.float32) + middle).astype(jnp.bfloat16)
        else:
            cotangent = (passed.astype(jnp.float32) + skip_terms[section_idx + 1].astype(jnp.float32)).astype(jnp.bfloat16)
        back_weight = jnp.flip(kernel_of(section_weight, section_idx), (0, 1)).transpose(0, 1, 3, 2).reshape(9 * C, C)
        summed = jnp.dot(patches(cotangent), back_weight, preferred_element_type=jnp.float32).reshape(cotangent.shape)
        slope_term = summed * silu_slope(pre_acts[section_idx])
        weight_grad = lax.dot_general(patches(activations[section_idx]), cotangent.reshape(-1, C), (((0,), (0,)), ((), ())), preferred_element_type=jnp.float32)
        section_grads.append(weight_grad.reshape(3, 3, C, C).transpose(3, 0, 1, 2).reshape(9 * C * C))
        passed = (cotangent.astype(jnp.float32) + slope_term).astype(jnp.bfloat16)
        if section_idx == HALF:
            middle = slope_term
        elif section_idx > HALF:
            skip_terms[SECTIONS - section_idx] = slope_term.astype(jnp.bfloat16)
    return jnp.stack(section_grads[::-1])
```

```python
import jax
import jax.numpy as jnp
from jax import lax
from jax.sharding import PartitionSpec as P


def silu_slope(pre_act):
    sigmoid = jax.nn.sigmoid(pre_act)
    return sigmoid * (1.0 + pre_act * (1.0 - sigmoid))


def conv(act, weight):
    return lax.conv_general_dilated(
        act, weight, (1, 1), ((1, 1), (1, 1)),
        dimension_numbers=("NHWC", "OHWI", "NHWC"),
        preferred_element_type=jnp.float32,
    )


def conv_t(cot, weight):
    flipped = jnp.flip(cot, (1, 2))
    out = lax.conv_general_dilated(
        flipped, weight, (1, 1), ((1, 1), (1, 1)),
        dimension_numbers=("NHWC", "IHWO", "NHWC"),
        preferred_element_type=jnp.float32,
    )
    return jnp.flip(out, (1, 2))


def weight_grad(act, cot):
    return lax.conv_general_dilated(
        act, cot, (1, 1), ((1, 1), (1, 1)),
        dimension_numbers=("CHWN", "IHWO", "CHWN"),
        preferred_element_type=jnp.float32,
    )


def f32(v):
    return v.astype(jnp.float32)


def bf16(v):
    return v.astype(jnp.bfloat16)


def local(latent, section_weight, out_grad):
    pipe_size = lax.axis_size("pipe")
    half = pipe_size // 2
    device = lax.axis_index("pipe")
    lower = device < half
    stage = jnp.minimum(device, pipe_size - 1 - device)
    mp_size = lax.axis_size("mp")
    lane = lax.axis_index("mp")

    channels = latent.shape[-1]
    img = latent.shape[-3:]
    samples = latent.reshape((-1,) + img)
    grads = out_grad.reshape((-1,) + img)
    per_lane = samples.shape[0] // mp_size
    x0 = lax.dynamic_slice_in_dim(samples, lane * per_lane, per_lane, 0)
    seed = lax.dynamic_slice_in_dim(grads, lane * per_lane, per_lane, 0)

    chan_half = section_weight.shape[-1] // (9 * channels)
    full = lax.all_gather(section_weight[0], "mp", axis=1, tiled=True)
    out_channels = chan_half * mp_size
    w_enc = full[0].reshape(out_channels, 3, 3, channels)
    w_dec = full[1].reshape(out_channels, 3, 3, channels)

    def up(t, v):
        pairs = [(t, t + 1), (pipe_size - 1 - t, pipe_size - 2 - t)]
        return lax.ppermute(v, "pipe", pairs)

    def down(t, v):
        pairs = [(t, t - 1), (pipe_size - 1 - t, pipe_size - t)]
        return lax.ppermute(v, "pipe", pairs)

    u0 = f32(x0)
    a0 = bf16(jax.nn.silu(u0))
    h1 = bf16(u0 + conv(a0, w_enc))
    d_last = conv_t(seed, w_dec)
    h1_r = up(0, h1)
    d_last_r = up(0, d_last)

    enc_in, enc_act, enc_out = {}, {}, {}
    enc_in[0], enc_act[0], enc_out[0] = x0, a0, h1
    received = h1_r
    for t in range(1, half):
        h_in = received
        u = f32(h_in)
        a = bf16(jax.nn.silu(u))
        h_out = bf16(u + conv(a, w_enc))
        enc_in[t], enc_act[t], enc_out[t] = h_in, a, h_out
        if t < half - 1:
            received = up(t, h_out)

    dec_u, dec_act, dec_c = {}, {}, {}
    h_in = enc_out[half - 1]
    u = f32(h_in) + f32(h_in)
    a = bf16(jax.nn.silu(u))
    current = bf16(f32(h_in) + conv(a, w_dec))
    dec_u[half - 1], dec_act[half - 1] = u, a
    for t in range(half - 2, 0, -1):
        h_in = down(t + 1, current)
        u = f32(h_in) + f32(enc_out[t])
        a = bf16(jax.nn.silu(u))
        current = bf16(f32(h_in) + conv(a, w_dec))
        dec_u[t], dec_act[t] = u, a

    u_last = f32(current) + f32(h1_r)
    a_last = bf16(jax.nn.silu(u_last))
    b_last = d_last_r * silu_slope(u_last)
    skip = {1: bf16(b_last)}
    a_last_r = lax.ppermute(a_last, "pipe", [(pipe_size - 2, pipe_size - 1)])
    cot = bf16(f32(seed) + b_last)

    for t in range(1, half):
        if t > 1:
            cot = up(t - 1, cot)
        dec_c[t] = cot
        d = conv_t(cot, w_dec)
        b = d * silu_slope(dec_u[t])
        g = bf16(f32(cot) + b)
        if t < half - 1:
            skip[t + 1] = bf16(b)
            cot = g
        else:
            cot = bf16(f32(g) + b)

    enc_c = {}
    for t in range(half - 1, 0, -1):
        if t < half - 1:
            cot = bf16(f32(down(t + 1, cot)) + f32(skip[t + 1]))
        enc_c[t] = cot
        d = conv_t(cot, w_enc)
        b = d * silu_slope(f32(enc_in[t]))
        cot = bf16(f32(cot) + b)
    c0 = bf16(f32(cot) + f32(skip[1]))
    c0_r = lax.ppermute(c0, "pipe", [(1, 0)])

    acts_lo = jnp.stack([a0] + [enc_act[t] for t in range(1, half)])
    cots_lo = jnp.stack([c0_r] + [enc_c[t] for t in range(1, half)])
    acts_up = jnp.stack([a_last_r] + [dec_act[t] for t in range(1, half)])
    cots_up = jnp.stack([seed] + [dec_c[t] for t in range(1, half)])
    act_sel = jnp.where(lower, acts_lo[stage], acts_up[stage])
    cot_sel = jnp.where(lower, cots_lo[stage], cots_up[stage])

    both = jnp.concatenate([act_sel, cot_sel], axis=-1)
    every = lax.all_gather(both, ("dp", "mp"), axis=0, tiled=True)
    act_all = every[..., :channels]
    cot_all = lax.dynamic_slice_in_dim(every, channels + lane * chan_half, chan_half, 3)
    grad = weight_grad(act_all, cot_all)
    return grad.reshape(1, -1)


def solution(mesh):
    return jax.shard_map(
        local,
        mesh=mesh,
        in_specs=(
            P(("groups", "dp"), None, None, None, None, None),
            P("pipe", None, "mp"),
            P(("groups", "dp"), None, None, None, None, None),
        ),
        out_specs=P(("groups", "pipe"), "mp"),
        check_vma=False,
    )
```

```python
import jax
import jax.numpy as jnp
from jax import lax
from jax.sharding import PartitionSpec as P


def silu_slope(pre_act):
    sigmoid = jax.nn.sigmoid(pre_act)
    return sigmoid * (1.0 + pre_act * (1.0 - sigmoid))


def conv(act, weight):
    return lax.conv_general_dilated(
        act, weight, (1, 1), ((1, 1), (1, 1)),
        dimension_numbers=("NHWC", "OHWI", "NHWC"),
        preferred_element_type=jnp.float32,
    )


def conv_t(cot, weight):
    flipped = jnp.flip(cot, (1, 2))
    out = lax.conv_general_dilated(
        flipped, weight, (1, 1), ((1, 1), (1, 1)),
        dimension_numbers=("NHWC", "IHWO", "NHWC"),
        preferred_element_type=jnp.float32,
    )
    return jnp.flip(out, (1, 2))


def weight_grad(act, cot):
    return lax.conv_general_dilated(
        act, cot, (1, 1), ((1, 1), (1, 1)),
        dimension_numbers=("CHWN", "IHWO", "CHWN"),
        preferred_element_type=jnp.float32,
    )


def f32(v):
    return v.astype(jnp.float32)


def bf16(v):
    return v.astype(jnp.bfloat16)


def local(latent, section_weight, out_grad):
    pipe_size = lax.axis_size("pipe")
    half = pipe_size // 2
    device = lax.axis_index("pipe")
    lower = device < half
    stage = jnp.minimum(device, pipe_size - 1 - device)
    mp_size = lax.axis_size("mp")
    lane = lax.axis_index("mp")

    channels = latent.shape[-1]
    img = latent.shape[-3:]
    samples = latent.reshape((-1,) + img)
    grads = out_grad.reshape((-1,) + img)
    per_lane = samples.shape[0] // mp_size
    x0 = lax.dynamic_slice_in_dim(samples, lane * per_lane, per_lane, 0)
    seed = lax.dynamic_slice_in_dim(grads, lane * per_lane, per_lane, 0)

    chan_half = section_weight.shape[-1] // (9 * channels)
    halves = section_weight[0].reshape(2, chan_half, 3, 3, channels)
    full = lax.all_gather(halves, "mp", axis=1, tiled=True)
    w_enc, w_dec = full[0], full[1]

    def up(t, v):
        pairs = [(t, t + 1), (pipe_size - 1 - t, pipe_size - 2 - t)]
        return lax.ppermute(v, "pipe", pairs)

    def down(t, v):
        pairs = [(t, t - 1), (pipe_size - 1 - t, pipe_size - t)]
        return lax.ppermute(v, "pipe", pairs)

    u0 = f32(x0)
    a0 = bf16(jax.nn.silu(u0))
    h1 = bf16(u0 + conv(a0, w_enc))
    d_last = conv_t(seed, w_dec)
    h1_r = up(0, h1)
    d_last_r = up(0, d_last)

    enc_in, enc_act, enc_out = {}, {}, {}
    enc_in[0], enc_act[0], enc_out[0] = x0, a0, h1
    received = h1_r
    for t in range(1, half):
        h_in = received
        u = f32(h_in)
        a = bf16(jax.nn.silu(u))
        h_out = bf16(u + conv(a, w_enc))
        enc_in[t], enc_act[t], enc_out[t] = h_in, a, h_out
        if t < half - 1:
            received = up(t, h_out)

    dec_u, dec_act, dec_c = {}, {}, {}
    h_in = enc_out[half - 1]
    u = f32(h_in) + f32(h_in)
    a = bf16(jax.nn.silu(u))
    current = bf16(f32(h_in) + conv(a, w_dec))
    dec_u[half - 1], dec_act[half - 1] = u, a
    for t in range(half - 2, 0, -1):
        h_in = down(t + 1, current)
        u = f32(h_in) + f32(enc_out[t])
        a = bf16(jax.nn.silu(u))
        current = bf16(f32(h_in) + conv(a, w_dec))
        dec_u[t], dec_act[t] = u, a

    u_last = f32(current) + f32(h1_r)
    a_last = bf16(jax.nn.silu(u_last))
    b_last = d_last_r * silu_slope(u_last)
    skip = {1: bf16(b_last)}
    a_last_r = lax.ppermute(a_last, "pipe", [(pipe_size - 2, pipe_size - 1)])
    cot = bf16(f32(seed) + b_last)

    for t in range(1, half):
        if t > 1:
            cot = up(t - 1, cot)
        dec_c[t] = cot
        d = conv_t(cot, w_dec)
        b = d * silu_slope(dec_u[t])
        g = bf16(f32(cot) + b)
        if t < half - 1:
            skip[t + 1] = bf16(b)
            cot = g
        else:
            cot = bf16(f32(g) + b)

    enc_c = {}
    for t in range(half - 1, 0, -1):
        if t < half - 1:
            cot = bf16(f32(down(t + 1, cot)) + f32(skip[t + 1]))
        enc_c[t] = cot
        d = conv_t(cot, w_enc)
        b = d * silu_slope(f32(enc_in[t]))
        cot = bf16(f32(cot) + b)
    c0 = bf16(f32(cot) + f32(skip[1]))
    c0_r = lax.ppermute(c0, "pipe", [(1, 0)])

    acts_lo = jnp.stack([a0] + [enc_act[t] for t in range(1, half)])
    cots_lo = jnp.stack([c0_r] + [enc_c[t] for t in range(1, half)])
    acts_up = jnp.stack([a_last_r] + [dec_act[t] for t in range(1, half)])
    cots_up = jnp.stack([seed] + [dec_c[t] for t in range(1, half)])
    act_sel = jnp.where(lower, acts_lo[stage], acts_up[stage])
    cot_sel = jnp.where(lower, cots_lo[stage], cots_up[stage])

    both = jnp.concatenate([act_sel, cot_sel], axis=-1)
    every = lax.all_gather(both, ("dp", "mp"), axis=0, tiled=True)
    act_all = every[..., :channels]
    cot_all = lax.dynamic_slice_in_dim(every, channels + lane * chan_half, chan_half, 3)
    grad = weight_grad(act_all, cot_all)
    return grad.reshape(1, -1)


def solution(mesh):
    return jax.shard_map(
        local,
        mesh=mesh,
        in_specs=(
            P(("groups", "dp"), None, None, None, None, None),
            P("pipe", None, "mp"),
            P(("groups", "dp"), None, None, None, None, None),
        ),
        out_specs=P(("groups", "pipe"), "mp"),
        check_vma=False,
    )
```

```python
import jax
import jax.numpy as jnp
from jax import lax
from jax.sharding import PartitionSpec as P


def silu_slope(pre_act):
    sigmoid = jax.nn.sigmoid(pre_act)
    return sigmoid * (1.0 + pre_act * (1.0 - sigmoid))


def conv(act, weight):
    return lax.conv_general_dilated(
        act, weight, (1, 1), ((1, 1), (1, 1)),
        dimension_numbers=("NHWC", "OHWI", "NHWC"),
        preferred_element_type=jnp.float32,
    )


def conv_t(cot, weight):
    flipped = jnp.flip(cot, (1, 2))
    out = lax.conv_general_dilated(
        flipped, weight, (1, 1), ((1, 1), (1, 1)),
        dimension_numbers=("NHWC", "IHWO", "NHWC"),
        preferred_element_type=jnp.float32,
    )
    return jnp.flip(out, (1, 2))


def weight_grad(act, cot):
    return lax.conv_general_dilated(
        act, cot, (1, 1), ((1, 1), (1, 1)),
        dimension_numbers=("CHWN", "IHWO", "CHWN"),
        preferred_element_type=jnp.float32,
    )


def f32(v):
    return v.astype(jnp.float32)


def bf16(v):
    return v.astype(jnp.bfloat16)


def lane_shift(v, dd, dm):
    nd, nm = lax.axis_size("dp"), lax.axis_size("mp")
    pairs = [
        (((d + dd) % nd) * nm + (m + dm) % nm, d * nm + m)
        for d in range(nd)
        for m in range(nm)
    ]
    return lax.ppermute(v, ("dp", "mp"), pairs)


def cross_shift(v, dd, dm):
    npipe, nd, nm = lax.axis_size("pipe"), lax.axis_size("dp"), lax.axis_size("mp")
    pairs = []
    for src, dst in ((1, 0), (npipe - 2, npipe - 1)):
        for d in range(nd):
            for m in range(nm):
                source = (src * nd + (d + dd) % nd) * nm + (m + dm) % nm
                pairs.append((source, (dst * nd + d) * nm + m))
    return lax.ppermute(v, ("pipe", "dp", "mp"), pairs)


def every_lane(v, shift):
    nd, nm = lax.axis_size("dp"), lax.axis_size("mp")
    parts = [shift(v, dd, dm) if (dd, dm) != (0, 0) or shift is cross_shift else v
             for dd in range(nd) for dm in range(nm)]
    return jnp.concatenate(parts, axis=0)


def local(latent, section_weight, out_grad):
    pipe_size = lax.axis_size("pipe")
    half = pipe_size // 2
    device = lax.axis_index("pipe")
    lower = device < half
    stage = jnp.minimum(device, pipe_size - 1 - device)
    lane = lax.axis_index("mp")
    swap = [(0, 1), (1, 0)]

    channels = latent.shape[-1]
    img = latent.shape[-3:]
    samples = latent.reshape((-1,) + img)
    grads = out_grad.reshape((-1,) + img)
    per_lane = samples.shape[0] // 2
    mine = lane * per_lane
    theirs = (1 - lane) * per_lane

    chan_half = section_weight.shape[-1] // (9 * channels)
    own = section_weight[0].reshape(2, chan_half, 3, 3, channels)
    other = lax.ppermute(own, "mp", swap)

    def up(t, v):
        pairs = [(t, t + 1), (pipe_size - 1 - t, pipe_size - 2 - t)]
        return lax.ppermute(v, "pipe", pairs)

    def down(t, v):
        pairs = [(t, t - 1), (pipe_size - 1 - t, pipe_size - t)]
        return lax.ppermute(v, "pipe", pairs)

    def take(v, at):
        return lax.dynamic_slice_in_dim(v, at, per_lane, 0)

    def join(first, second):
        return jnp.where(lane == 0, jnp.concatenate([first, second], -1),
                         jnp.concatenate([second, first], -1))

    low = lane * chan_half
    act_all = bf16(jax.nn.silu(f32(samples)))
    own_in = lax.dynamic_slice_in_dim(samples, low, chan_half, 3)
    h1_half = bf16(f32(own_in) + conv(act_all, own[0]))
    seed_half = lax.dynamic_slice_in_dim(grads, low, chan_half, 3)
    d_part = conv_t(seed_half, own[1])
    h1_got, d_got = lax.ppermute((take(h1_half, theirs), take(d_part, theirs)), "mp", swap)
    h1 = join(take(h1_half, mine), h1_got)
    d_last = take(d_part, mine) + d_got
    x0 = take(samples, mine)
    a0 = take(act_all, mine)
    seed = take(grads, mine)
    h1_r = up(0, h1)
    d_last_r = up(0, d_last)

    other, _ = lax.optimization_barrier((other, h1))
    full = jnp.where(lane == 0, jnp.concatenate([own, other], 1),
                     jnp.concatenate([other, own], 1))
    w_enc, w_dec = full[0], full[1]

    enc_in, enc_act, enc_out = {}, {}, {}
    enc_in[0], enc_act[0], enc_out[0] = x0, a0, h1
    received = h1_r
    for t in range(1, half):
        h_in = received
        u = f32(h_in)
        a = bf16(jax.nn.silu(u))
        h_out = bf16(u + conv(a, w_enc))
        enc_in[t], enc_act[t], enc_out[t] = h_in, a, h_out
        if t < half - 1:
            received = up(t, h_out)

    dec_u, dec_act, dec_c = {}, {}, {}
    h_in = enc_out[half - 1]
    u = f32(h_in) + f32(h_in)
    a = bf16(jax.nn.silu(u))
    current = bf16(f32(h_in) + conv(a, w_dec))
    dec_u[half - 1], dec_act[half - 1] = u, a
    for t in range(half - 2, 0, -1):
        h_in = down(t + 1, current)
        u = f32(h_in) + f32(enc_out[t])
        a = bf16(jax.nn.silu(u))
        current = bf16(f32(h_in) + conv(a, w_dec))
        dec_u[t], dec_act[t] = u, a

    u_last = f32(current) + f32(h1_r)
    a_last = bf16(jax.nn.silu(u_last))
    b_last = d_last_r * silu_slope(u_last)
    skip = {1: bf16(b_last)}
    cot = bf16(f32(seed) + b_last)

    for t in range(1, half):
        if t > 1:
            cot = up(t - 1, cot)
        dec_c[t] = cot
        d = conv_t(cot, w_dec)
        b = d * silu_slope(dec_u[t])
        g = bf16(f32(cot) + b)
        if t < half - 1:
            skip[t + 1] = bf16(b)
            cot = g
        else:
            cot = bf16(f32(g) + b)

    enc_c = {}
    for t in range(half - 1, 0, -1):
        if t < half - 1:
            cot = bf16(f32(down(t + 1, cot)) + f32(skip[t + 1]))
        enc_c[t] = cot
        d = conv_t(cot, w_enc)
        b = d * silu_slope(f32(enc_in[t]))
        cot = bf16(f32(cot) + b)
    c0 = bf16(f32(cot) + f32(skip[1]))

    late = every_lane(jnp.concatenate([jnp.where(lower, c0, a_last)], -1), cross_shift)
    early = every_lane(jnp.concatenate([a0, seed], -1), lane_shift)
    acts = jnp.stack([enc_act[t] for t in range(1, half)] or [a0])
    cots = jnp.stack([enc_c[t] for t in range(1, half)] or [a0])
    acts_up = jnp.stack([dec_act[t] for t in range(1, half)] or [a0])
    cots_up = jnp.stack([dec_c[t] for t in range(1, half)] or [a0])
    at = jnp.maximum(stage - 1, 0)
    mid = every_lane(
        jnp.concatenate([jnp.where(lower, acts[at], acts_up[at]),
                         jnp.where(lower, cots[at], cots_up[at])], -1),
        lane_shift)
    first_a = jnp.where(lower, early[..., :channels], late)
    first_c = jnp.where(lower, late, early[..., channels:])
    act_all = jnp.where(stage == 0, first_a, mid[..., :channels])
    cot_all = jnp.where(stage == 0, first_c, mid[..., channels:])
    cot_all = lax.dynamic_slice_in_dim(cot_all, low, chan_half, 3)
    grad = weight_grad(act_all, cot_all)
    return grad.reshape(1, -1)


def solution(mesh):
    return jax.shard_map(
        local,
        mesh=mesh,
        in_specs=(
            P(("groups", "dp"), None, None, None, None, None),
            P("pipe", None, "mp"),
            P(("groups", "dp"), None, None, None, None, None),
        ),
        out_specs=P(("groups", "pipe"), "mp"),
        check_vma=False,
    )
```

```python
import jax
import jax.numpy as jnp
from jax import lax
from jax.sharding import PartitionSpec as P


def silu_slope(pre_act):
    sigmoid = jax.nn.sigmoid(pre_act)
    return sigmoid * (1.0 + pre_act * (1.0 - sigmoid))


def conv(act, weight):
    return lax.conv_general_dilated(
        act, weight, (1, 1), ((1, 1), (1, 1)),
        dimension_numbers=("NHWC", "OHWI", "NHWC"),
        preferred_element_type=jnp.float32,
    )


def conv_t(cot, weight):
    flipped = jnp.flip(cot, (1, 2))
    out = lax.conv_general_dilated(
        flipped, weight, (1, 1), ((1, 1), (1, 1)),
        dimension_numbers=("NHWC", "IHWO", "NHWC"),
        preferred_element_type=jnp.float32,
    )
    return jnp.flip(out, (1, 2))


def weight_grad(act, cot):
    return lax.conv_general_dilated(
        act, cot, (1, 1), ((1, 1), (1, 1)),
        dimension_numbers=("CHWN", "IHWO", "CHWN"),
        preferred_element_type=jnp.float32,
    )


def f32(v):
    return v.astype(jnp.float32)


def bf16(v):
    return v.astype(jnp.bfloat16)


def local(latent, section_weight, out_grad):
    pipe_size = lax.axis_size("pipe")
    half = pipe_size // 2
    device = lax.axis_index("pipe")
    lower = device < half
    stage = jnp.minimum(device, pipe_size - 1 - device)
    lane = lax.axis_index("mp")
    swap = [(0, 1), (1, 0)]

    channels = latent.shape[-1]
    img = latent.shape[-3:]
    samples = latent.reshape((-1,) + img)
    grads = out_grad.reshape((-1,) + img)
    per_lane = samples.shape[0] // 2
    mine = lane * per_lane
    theirs = (1 - lane) * per_lane

    chan_half = section_weight.shape[-1] // (9 * channels)
    own = lax.optimization_barrier(section_weight[0].reshape(2, chan_half, 3, 3, channels))
    other = lax.ppermute(own, "mp", swap)

    def up(t, v):
        pairs = [(t, t + 1), (pipe_size - 1 - t, pipe_size - 2 - t)]
        return lax.ppermute(v, "pipe", pairs)

    def down(t, v):
        pairs = [(t, t - 1), (pipe_size - 1 - t, pipe_size - t)]
        return lax.ppermute(v, "pipe", pairs)

    def take(v, at):
        return lax.dynamic_slice_in_dim(v, at, per_lane, 0)

    def join(first, second):
        return jnp.where(lane == 0, jnp.concatenate([first, second], -1),
                         jnp.concatenate([second, first], -1))

    low = lane * chan_half
    act_all = bf16(jax.nn.silu(f32(samples)))
    own_in = lax.dynamic_slice_in_dim(samples, low, chan_half, 3)
    h1_half = bf16(f32(own_in) + conv(act_all, own[0]))
    seed_half = lax.dynamic_slice_in_dim(grads, low, chan_half, 3)
    d_part = conv_t(seed_half, own[1])
    h1_got, d_got = lax.ppermute((take(h1_half, theirs), take(d_part, theirs)), "mp", swap)
    h1 = join(take(h1_half, mine), h1_got)
    d_last = take(d_part, mine) + d_got
    x0 = take(samples, mine)
    a0 = take(act_all, mine)
    seed = take(grads, mine)
    h1_r = up(0, h1)
    d_last_r = up(0, d_last)

    other, _ = lax.optimization_barrier((other, h1))
    full = jnp.where(lane == 0, jnp.concatenate([own, other], 1),
                     jnp.concatenate([other, own], 1))
    w_enc, w_dec = full[0], full[1]

    enc_in, enc_act, enc_out = {}, {}, {}
    enc_in[0], enc_act[0], enc_out[0] = x0, a0, h1
    received = h1_r
    for t in range(1, half):
        h_in = received
        u = f32(h_in)
        a = bf16(jax.nn.silu(u))
        h_out = bf16(u + conv(a, w_enc))
        enc_in[t], enc_act[t], enc_out[t] = h_in, a, h_out
        if t < half - 1:
            received = up(t, h_out)

    dec_u, dec_act, dec_c = {}, {}, {}
    h_in = enc_out[half - 1]
    u = f32(h_in) + f32(h_in)
    a = bf16(jax.nn.silu(u))
    current = bf16(f32(h_in) + conv(a, w_dec))
    dec_u[half - 1], dec_act[half - 1] = u, a
    for t in range(half - 2, 0, -1):
        h_in = down(t + 1, current)
        u = f32(h_in) + f32(enc_out[t])
        a = bf16(jax.nn.silu(u))
        current = bf16(f32(h_in) + conv(a, w_dec))
        dec_u[t], dec_act[t] = u, a

    u_last = f32(current) + f32(h1_r)
    a_last = bf16(jax.nn.silu(u_last))
    b_last = d_last_r * silu_slope(u_last)
    skip = {1: bf16(b_last)}
    cot = bf16(f32(seed) + b_last)

    for t in range(1, half):
        if t > 1:
            cot = up(t - 1, cot)
        dec_c[t] = cot
        d = conv_t(cot, w_dec)
        b = d * silu_slope(dec_u[t])
        g = bf16(f32(cot) + b)
        if t < half - 1:
            skip[t + 1] = bf16(b)
            cot = g
        else:
            cot = bf16(f32(g) + b)

    enc_c = {}
    for t in range(half - 1, 0, -1):
        if t < half - 1:
            cot = bf16(f32(down(t + 1, cot)) + f32(skip[t + 1]))
        enc_c[t] = cot
        d = conv_t(cot, w_enc)
        b = d * silu_slope(f32(enc_in[t]))
        cot = bf16(f32(cot) + b)
    c0 = bf16(f32(cot) + f32(skip[1]))

    sent = lax.ppermute(jnp.where(lower, c0, a_last), "pipe", [(1, 0), (pipe_size - 2, pipe_size - 1)])
    acts_lo = jnp.stack([a0] + [enc_act[t] for t in range(1, half)])
    cots_lo = jnp.stack([sent] + [enc_c[t] for t in range(1, half)])
    acts_up = jnp.stack([sent] + [dec_act[t] for t in range(1, half)])
    cots_up = jnp.stack([seed] + [dec_c[t] for t in range(1, half)])
    act_sel = jnp.where(lower, acts_lo[stage], acts_up[stage])
    cot_sel = jnp.where(lower, cots_lo[stage], cots_up[stage])
    both = jnp.concatenate([act_sel, cot_sel], axis=-1)
    every = lax.all_gather(both, ("dp", "mp"), axis=0, tiled=True)
    act_all = every[..., :channels]
    cot_all = lax.dynamic_slice_in_dim(every, channels + low, chan_half, 3)
    grad = weight_grad(act_all, cot_all)
    return grad.reshape(1, -1)


def solution(mesh):
    return jax.shard_map(
        local,
        mesh=mesh,
        in_specs=(
            P(("groups", "dp"), None, None, None, None, None),
            P("pipe", None, "mp"),
            P(("groups", "dp"), None, None, None, None, None),
        ),
        out_specs=P(("groups", "pipe"), "mp"),
        check_vma=False,
    )
```

```python
import jax
import jax.numpy as jnp
from jax import lax
from jax.sharding import PartitionSpec as P


def silu_slope(pre_act):
    sigmoid = jax.nn.sigmoid(pre_act)
    return sigmoid * (1.0 + pre_act * (1.0 - sigmoid))


def conv(act, weight):
    return lax.conv_general_dilated(
        act, weight, (1, 1), ((1, 1), (1, 1)),
        dimension_numbers=("NHWC", "OHWI", "NHWC"),
        preferred_element_type=jnp.float32,
    )


def conv_t(cot, weight):
    flipped = jnp.flip(cot, (1, 2))
    out = lax.conv_general_dilated(
        flipped, weight, (1, 1), ((1, 1), (1, 1)),
        dimension_numbers=("NHWC", "IHWO", "NHWC"),
        preferred_element_type=jnp.float32,
    )
    return jnp.flip(out, (1, 2))


def weight_grad(act, cot):
    return lax.conv_general_dilated(
        act, cot, (1, 1), ((1, 1), (1, 1)),
        dimension_numbers=("CHWN", "IHWO", "CHWN"),
        preferred_element_type=jnp.float32,
    )


def f32(v):
    return v.astype(jnp.float32)


def bf16(v):
    return v.astype(jnp.bfloat16)


def local(latent, section_weight, out_grad):
    pipe_size = lax.axis_size("pipe")
    half = pipe_size // 2
    device = lax.axis_index("pipe")
    lower = device < half
    stage = jnp.minimum(device, pipe_size - 1 - device)
    lane = lax.axis_index("mp")
    swap = [(0, 1), (1, 0)]

    channels = latent.shape[-1]
    img = latent.shape[-3:]
    samples = latent.reshape((-1,) + img)
    grads = out_grad.reshape((-1,) + img)
    per_lane = samples.shape[0] // 2
    mine = lane * per_lane
    theirs = (1 - lane) * per_lane

    chan_half = section_weight.shape[-1] // (9 * channels)
    own = lax.optimization_barrier(
        section_weight[0].reshape(2, chan_half, 9, channels).transpose(0, 2, 1, 3)
        .reshape(2, 3, 3, chan_half, channels)
    ).transpose(0, 3, 1, 2, 4)
    other = lax.ppermute(own, "mp", swap)

    def up(t, v):
        pairs = [(t, t + 1), (pipe_size - 1 - t, pipe_size - 2 - t)]
        return lax.ppermute(v, "pipe", pairs)

    def down(t, v):
        pairs = [(t, t - 1), (pipe_size - 1 - t, pipe_size - t)]
        return lax.ppermute(v, "pipe", pairs)

    def take(v, at):
        return lax.dynamic_slice_in_dim(v, at, per_lane, 0)

    def join(first, second):
        return jnp.where(lane == 0, jnp.concatenate([first, second], -1),
                         jnp.concatenate([second, first], -1))

    low = lane * chan_half
    act_all = bf16(jax.nn.silu(f32(samples)))
    own_in = lax.dynamic_slice_in_dim(samples, low, chan_half, 3)
    h1_half = bf16(f32(own_in) + conv(act_all, own[0]))
    seed_half = lax.dynamic_slice_in_dim(grads, low, chan_half, 3)
    d_part = conv_t(seed_half, own[1])
    h1_all = lax.all_gather(h1_half, "mp", axis=3, tiled=False)
    d_all = lax.all_gather(d_part, "mp", axis=0, tiled=False)
    h1 = take(jnp.concatenate([h1_all[..., 0, :], h1_all[..., 1, :]], -1), mine)
    d_last = take(d_all[0] + d_all[1], mine)
    x0 = take(samples, mine)
    a0 = take(act_all, mine)
    seed = take(grads, mine)
    h1_r = up(0, h1)
    d_last_r = up(0, d_last)

    other, _ = lax.optimization_barrier((other, h1))
    full = jnp.where(lane == 0, jnp.concatenate([own, other], 1),
                     jnp.concatenate([other, own], 1))
    w_enc, w_dec = full[0], full[1]

    enc_in, enc_act, enc_out = {}, {}, {}
    enc_in[0], enc_act[0], enc_out[0] = x0, a0, h1
    received = h1_r
    for t in range(1, half):
        h_in = received
        u = f32(h_in)
        a = bf16(jax.nn.silu(u))
        h_out = bf16(u + conv(a, w_enc))
        enc_in[t], enc_act[t], enc_out[t] = h_in, a, h_out
        if t < half - 1:
            received = up(t, h_out)

    dec_u, dec_act, dec_c = {}, {}, {}
    h_in = enc_out[half - 1]
    u = f32(h_in) + f32(h_in)
    a = bf16(jax.nn.silu(u))
    current = bf16(f32(h_in) + conv(a, w_dec))
    dec_u[half - 1], dec_act[half - 1] = u, a
    for t in range(half - 2, 0, -1):
        h_in = down(t + 1, current)
        u = f32(h_in) + f32(enc_out[t])
        a = bf16(jax.nn.silu(u))
        current = bf16(f32(h_in) + conv(a, w_dec))
        dec_u[t], dec_act[t] = u, a

    u_last = f32(current) + f32(h1_r)
    a_last = bf16(jax.nn.silu(u_last))
    b_last = d_last_r * silu_slope(u_last)
    skip = {1: bf16(b_last)}
    cot = bf16(f32(seed) + b_last)

    for t in range(1, half):
        if t > 1:
            cot = up(t - 1, cot)
        dec_c[t] = cot
        d = conv_t(cot, w_dec)
        b = d * silu_slope(dec_u[t])
        g = bf16(f32(cot) + b)
        if t < half - 1:
            skip[t + 1] = bf16(b)
            cot = g
        else:
            cot = bf16(f32(g) + b)

    enc_c = {}
    for t in range(half - 1, 0, -1):
        if t < half - 1:
            cot = bf16(f32(down(t + 1, cot)) + f32(skip[t + 1]))
        enc_c[t] = cot
        d = conv_t(cot, w_enc)
        b = d * silu_slope(f32(enc_in[t]))
        cot = bf16(f32(cot) + b)
    c0 = bf16(f32(cot) + f32(skip[1]))

    sent = lax.ppermute(jnp.where(lower, c0, a_last), "pipe", [(1, 0), (pipe_size - 2, pipe_size - 1)])
    acts_lo = jnp.stack([a0] + [enc_act[t] for t in range(1, half)])
    cots_lo = jnp.stack([sent] + [enc_c[t] for t in range(1, half)])
    acts_up = jnp.stack([sent] + [dec_act[t] for t in range(1, half)])
    cots_up = jnp.stack([seed] + [dec_c[t] for t in range(1, half)])
    act_sel = jnp.where(lower, acts_lo[stage], acts_up[stage])
    cot_sel = jnp.where(lower, cots_lo[stage], cots_up[stage])
    both = jnp.concatenate([act_sel, cot_sel], axis=-1)
    every = lax.all_gather(both, ("dp", "mp"), axis=0, tiled=True)
    act_all = every[..., :channels]
    cot_all = lax.dynamic_slice_in_dim(every, channels + low, chan_half, 3)
    grad = weight_grad(act_all, cot_all)
    return grad.reshape(1, -1)


def solution(mesh):
    return jax.shard_map(
        local,
        mesh=mesh,
        in_specs=(
            P(("groups", "dp"), None, None, None, None, None),
            P("pipe", None, "mp"),
            P(("groups", "dp"), None, None, None, None, None),
        ),
        out_specs=P(("groups", "pipe"), "mp"),
        check_vma=False,
    )
```

```python
import jax
import jax.numpy as jnp
from jax import lax
from jax.sharding import PartitionSpec as P


def silu_slope(pre_act):
    sigmoid = jax.nn.sigmoid(pre_act)
    return sigmoid * (1.0 + pre_act * (1.0 - sigmoid))


def conv(act, weight):
    return lax.conv_general_dilated(
        act, weight, (1, 1), ((1, 1), (1, 1)),
        dimension_numbers=("NHWC", "OHWI", "NHWC"),
        preferred_element_type=jnp.float32,
    )


def conv_t(cot, weight):
    flipped = jnp.flip(cot, (1, 2))
    out = lax.conv_general_dilated(
        flipped, weight, (1, 1), ((1, 1), (1, 1)),
        dimension_numbers=("NHWC", "IHWO", "NHWC"),
        preferred_element_type=jnp.float32,
    )
    return jnp.flip(out, (1, 2))


def weight_grad(act, cot):
    return lax.conv_general_dilated(
        act, cot, (1, 1), ((1, 1), (1, 1)),
        dimension_numbers=("CHWN", "IHWO", "CHWN"),
        preferred_element_type=jnp.float32,
    )


def f32(v):
    return v.astype(jnp.float32)


def bf16(v):
    return v.astype(jnp.bfloat16)


def local_general(latent, section_weight, out_grad):
    pipe_size = lax.axis_size("pipe")
    half = pipe_size // 2
    device = lax.axis_index("pipe")
    lower = device < half
    stage = jnp.minimum(device, pipe_size - 1 - device)
    lane = lax.axis_index("mp")
    swap = [(0, 1), (1, 0)]

    channels = latent.shape[-1]
    img = latent.shape[-3:]
    samples = latent.reshape((-1,) + img)
    grads = out_grad.reshape((-1,) + img)
    per_lane = samples.shape[0] // 2
    mine = lane * per_lane
    theirs = (1 - lane) * per_lane

    chan_half = section_weight.shape[-1] // (9 * channels)
    own = lax.optimization_barrier(
        section_weight[0].reshape(2, chan_half, 9, channels).transpose(0, 2, 1, 3)
        .reshape(2, 3, 3, chan_half, channels)
    ).transpose(0, 3, 1, 2, 4)
    other = lax.ppermute(own, "mp", swap)

    def up(t, v):
        pairs = [(t, t + 1), (pipe_size - 1 - t, pipe_size - 2 - t)]
        return lax.ppermute(v, "pipe", pairs)

    def down(t, v):
        pairs = [(t, t - 1), (pipe_size - 1 - t, pipe_size - t)]
        return lax.ppermute(v, "pipe", pairs)

    def take(v, at):
        return lax.dynamic_slice_in_dim(v, at, per_lane, 0)

    def join(first, second):
        return jnp.where(lane == 0, jnp.concatenate([first, second], -1),
                         jnp.concatenate([second, first], -1))

    low = lane * chan_half
    act_all = bf16(jax.nn.silu(f32(samples)))
    own_in = lax.dynamic_slice_in_dim(samples, low, chan_half, 3)
    h1_half = bf16(f32(own_in) + conv(act_all, own[0]))
    seed_half = lax.dynamic_slice_in_dim(grads, low, chan_half, 3)
    d_part = conv_t(seed_half, own[1])
    h1_all = lax.all_gather(h1_half, "mp", axis=3, tiled=False)
    d_all = lax.all_gather(d_part, "mp", axis=0, tiled=False)
    h1 = take(jnp.concatenate([h1_all[..., 0, :], h1_all[..., 1, :]], -1), mine)
    d_last = take(d_all[0] + d_all[1], mine)
    x0 = take(samples, mine)
    a0 = take(act_all, mine)
    seed = take(grads, mine)
    h1_r = up(0, h1)
    d_last_r = up(0, d_last)

    other, _ = lax.optimization_barrier((other, h1))
    full = jnp.where(lane == 0, jnp.concatenate([own, other], 1),
                     jnp.concatenate([other, own], 1))
    w_enc, w_dec = full[0], full[1]

    enc_in, enc_act, enc_out = {}, {}, {}
    enc_in[0], enc_act[0], enc_out[0] = x0, a0, h1
    received = h1_r
    for t in range(1, half):
        h_in = received
        u = f32(h_in)
        a = bf16(jax.nn.silu(u))
        h_out = bf16(u + conv(a, w_enc))
        enc_in[t], enc_act[t], enc_out[t] = h_in, a, h_out
        if t < half - 1:
            received = up(t, h_out)

    dec_u, dec_act, dec_c = {}, {}, {}
    h_in = enc_out[half - 1]
    u = f32(h_in) + f32(h_in)
    a = bf16(jax.nn.silu(u))
    current = bf16(f32(h_in) + conv(a, w_dec))
    dec_u[half - 1], dec_act[half - 1] = u, a
    for t in range(half - 2, 0, -1):
        h_in = down(t + 1, current)
        u = f32(h_in) + f32(enc_out[t])
        a = bf16(jax.nn.silu(u))
        current = bf16(f32(h_in) + conv(a, w_dec))
        dec_u[t], dec_act[t] = u, a

    u_last = f32(current) + f32(h1_r)
    a_last = bf16(jax.nn.silu(u_last))
    b_last = d_last_r * silu_slope(u_last)
    skip = {1: bf16(b_last)}
    cot = bf16(f32(seed) + b_last)

    for t in range(1, half):
        if t > 1:
            cot = up(t - 1, cot)
        dec_c[t] = cot
        d = conv_t(cot, w_dec)
        b = d * silu_slope(dec_u[t])
        g = bf16(f32(cot) + b)
        if t < half - 1:
            skip[t + 1] = bf16(b)
            cot = g
        else:
            cot = bf16(f32(g) + b)

    enc_c = {}
    for t in range(half - 1, 0, -1):
        if t < half - 1:
            cot = bf16(f32(down(t + 1, cot)) + f32(skip[t + 1]))
        enc_c[t] = cot
        d = conv_t(cot, w_enc)
        b = d * silu_slope(f32(enc_in[t]))
        cot = bf16(f32(cot) + b)
    c0 = bf16(f32(cot) + f32(skip[1]))

    sent = lax.ppermute(jnp.where(lower, c0, a_last), "pipe", [(1, 0), (pipe_size - 2, pipe_size - 1)])
    acts_lo = jnp.stack([a0] + [enc_act[t] for t in range(1, half)])
    cots_lo = jnp.stack([sent] + [enc_c[t] for t in range(1, half)])
    acts_up = jnp.stack([sent] + [dec_act[t] for t in range(1, half)])
    cots_up = jnp.stack([seed] + [dec_c[t] for t in range(1, half)])
    act_sel = jnp.where(lower, acts_lo[stage], acts_up[stage])
    cot_sel = jnp.where(lower, cots_lo[stage], cots_up[stage])
    both = jnp.concatenate([act_sel, cot_sel], axis=-1)
    every = lax.all_gather(both, ("dp", "mp"), axis=0, tiled=True)
    act_all = every[..., :channels]
    cot_all = lax.dynamic_slice_in_dim(every, channels + low, chan_half, 3)
    grad = weight_grad(act_all, cot_all)
    return grad.reshape(1, -1)


def on_stage(active, fn, *args):
    shapes = jax.eval_shape(fn, *args)
    def idle(*unused):
        return jax.tree.map(lambda v: jnp.zeros(v.shape, v.dtype), shapes)
    return lax.cond(active, fn, idle, *args)


def local(latent, section_weight, out_grad):
    pipe_size = lax.axis_size("pipe")
    half = pipe_size // 2
    if half != 2:
        return local_general(latent, section_weight, out_grad)
    device = lax.axis_index("pipe")
    lower = device < half
    stage = jnp.minimum(device, pipe_size - 1 - device)
    lane = lax.axis_index("mp")
    swap = [(0, 1), (1, 0)]

    channels = latent.shape[-1]
    img = latent.shape[-3:]
    samples = latent.reshape((-1,) + img)
    grads = out_grad.reshape((-1,) + img)
    per_lane = samples.shape[0] // 2
    mine = lane * per_lane
    chan_half = section_weight.shape[-1] // (9 * channels)
    low = lane * chan_half

    def take(v, at):
        return lax.dynamic_slice_in_dim(v, at, per_lane, 0)

    own = lax.optimization_barrier(
        section_weight[0].reshape(2, chan_half, 9, channels).transpose(0, 2, 1, 3)
        .reshape(2, 3, 3, chan_half, channels)
    ).transpose(0, 3, 1, 2, 4)

    x0 = take(samples, mine)
    seed = take(grads, mine)
    a0 = bf16(jax.nn.silu(f32(x0)))

    def first(samples, grads, own):
        act_all = bf16(jax.nn.silu(f32(samples)))
        own_in = lax.dynamic_slice_in_dim(samples, low, chan_half, 3)
        h1_half = bf16(f32(own_in) + conv(act_all, own[0]))
        seed_half = lax.dynamic_slice_in_dim(grads, low, chan_half, 3)
        d_part = conv_t(seed_half, own[1])
        h1_all = lax.all_gather(h1_half, "mp", axis=3, tiled=False)
        d_all = lax.all_gather(d_part, "mp", axis=0, tiled=False)
        h1 = take(jnp.concatenate([h1_all[..., 0, :], h1_all[..., 1, :]], -1), mine)
        return h1, take(d_all[0] + d_all[1], mine)

    def weights(own):
        other = lax.ppermute(own, "mp", swap)
        return jnp.where(lane == 0, jnp.concatenate([own, other], 1),
                         jnp.concatenate([other, own], 1))

    h1, d_last = on_stage(stage == 0, first, samples, grads, own)
    full = on_stage(stage == 1, weights, own)
    ups = [(0, 1), (pipe_size - 1, pipe_size - 2)]
    h1_r = lax.ppermute(h1, "pipe", ups)
    d_last_r = lax.ppermute(d_last, "pipe", ups)

    def middle(h1_r, d_last_r, seed, full, lower):
        w_enc, w_dec = full[0], full[1]
        u1 = f32(h1_r)
        a1 = bf16(jax.nn.silu(u1))
        h2 = bf16(u1 + conv(a1, w_enc))
        u2 = f32(h2) + f32(h2)
        a2 = bf16(jax.nn.silu(u2))
        h3 = bf16(f32(h2) + conv(a2, w_dec))
        u3 = f32(h3) + u1
        a3 = bf16(jax.nn.silu(u3))
        b3 = d_last_r * silu_slope(u3)
        c2 = bf16(f32(seed) + b3)
        b2 = conv_t(c2, w_dec) * silu_slope(u2)
        g2 = bf16(f32(c2) + b2)
        c1 = bf16(f32(g2) + b2)
        b1 = conv_t(c1, w_enc) * silu_slope(u1)
        g1 = bf16(f32(c1) + b1)
        c0 = bf16(f32(g1) + f32(bf16(b3)))
        return (jnp.where(lower, c0, a3), jnp.where(lower, a1, a2),
                jnp.where(lower, c1, c2))

    back, act1, cot1 = on_stage(stage == 1, middle, h1_r, d_last_r, seed, full, lower)
    sent = lax.ppermute(back, "pipe", [(1, 0), (pipe_size - 2, pipe_size - 1)])

    act_sel = jnp.where(stage == 0, jnp.where(lower, a0, sent), act1)
    cot_sel = jnp.where(stage == 0, jnp.where(lower, sent, seed), cot1)
    both = jnp.concatenate([act_sel, cot_sel], axis=-1)
    every = lax.all_gather(both, ("dp", "mp"), axis=0, tiled=True)
    act_all = every[..., :channels]
    cot_all = lax.dynamic_slice_in_dim(every, channels + low, chan_half, 3)
    grad = weight_grad(act_all, cot_all)
    return grad.reshape(1, -1)


def solution(mesh):
    return jax.shard_map(
        local,
        mesh=mesh,
        in_specs=(
            P(("groups", "dp"), None, None, None, None, None),
            P("pipe", None, "mp"),
            P(("groups", "dp"), None, None, None, None, None),
        ),
        out_specs=P(("groups", "pipe"), "mp"),
        check_vma=False,
    )
```

```python
import jax
import jax.numpy as jnp
from jax import lax
from jax.sharding import PartitionSpec as P


def silu_slope(pre_act):
    sigmoid = jax.nn.sigmoid(pre_act)
    return sigmoid * (1.0 + pre_act * (1.0 - sigmoid))


def conv(act, weight):
    return lax.conv_general_dilated(
        act, weight, (1, 1), ((1, 1), (1, 1)),
        dimension_numbers=("NHWC", "OHWI", "NHWC"),
        preferred_element_type=jnp.float32,
    )


def conv_t(cot, weight):
    flipped = jnp.flip(cot, (1, 2))
    out = lax.conv_general_dilated(
        flipped, weight, (1, 1), ((1, 1), (1, 1)),
        dimension_numbers=("NHWC", "IHWO", "NHWC"),
        preferred_element_type=jnp.float32,
    )
    return jnp.flip(out, (1, 2))


def weight_grad(act, cot):
    return lax.conv_general_dilated(
        act, cot, (1, 1), ((1, 1), (1, 1)),
        dimension_numbers=("CHWN", "IHWO", "CHWN"),
        preferred_element_type=jnp.float32,
    )


def f32(v):
    return v.astype(jnp.float32)


def bf16(v):
    return v.astype(jnp.bfloat16)


def local_general(latent, section_weight, out_grad):
    pipe_size = lax.axis_size("pipe")
    half = pipe_size // 2
    device = lax.axis_index("pipe")
    lower = device < half
    stage = jnp.minimum(device, pipe_size - 1 - device)
    lane = lax.axis_index("mp")
    swap = [(0, 1), (1, 0)]

    channels = latent.shape[-1]
    img = latent.shape[-3:]
    samples = latent.reshape((-1,) + img)
    grads = out_grad.reshape((-1,) + img)
    per_lane = samples.shape[0] // 2
    mine = lane * per_lane
    theirs = (1 - lane) * per_lane

    chan_half = section_weight.shape[-1] // (9 * channels)
    own = lax.optimization_barrier(
        section_weight[0].reshape(2, chan_half, 9, channels).transpose(0, 2, 1, 3)
        .reshape(2, 3, 3, chan_half, channels)
    ).transpose(0, 3, 1, 2, 4)
    other = lax.ppermute(own, "mp", swap)

    def up(t, v):
        pairs = [(t, t + 1), (pipe_size - 1 - t, pipe_size - 2 - t)]
        return lax.ppermute(v, "pipe", pairs)

    def down(t, v):
        pairs = [(t, t - 1), (pipe_size - 1 - t, pipe_size - t)]
        return lax.ppermute(v, "pipe", pairs)

    def take(v, at):
        return lax.dynamic_slice_in_dim(v, at, per_lane, 0)

    def join(first, second):
        return jnp.where(lane == 0, jnp.concatenate([first, second], -1),
                         jnp.concatenate([second, first], -1))

    low = lane * chan_half
    act_all = bf16(jax.nn.silu(f32(samples)))
    own_in = lax.dynamic_slice_in_dim(samples, low, chan_half, 3)
    h1_half = bf16(f32(own_in) + conv(act_all, own[0]))
    seed_half = lax.dynamic_slice_in_dim(grads, low, chan_half, 3)
    d_part = conv_t(seed_half, own[1])
    h1_all = lax.all_gather(h1_half, "mp", axis=3, tiled=False)
    d_all = lax.all_gather(d_part, "mp", axis=0, tiled=False)
    h1 = take(jnp.concatenate([h1_all[..., 0, :], h1_all[..., 1, :]], -1), mine)
    d_last = take(d_all[0] + d_all[1], mine)
    x0 = take(samples, mine)
    a0 = take(act_all, mine)
    seed = take(grads, mine)
    h1_r = up(0, h1)
    d_last_r = up(0, d_last)

    other, _ = lax.optimization_barrier((other, h1))
    full = jnp.where(lane == 0, jnp.concatenate([own, other], 1),
                     jnp.concatenate([other, own], 1))
    w_enc, w_dec = full[0], full[1]

    enc_in, enc_act, enc_out = {}, {}, {}
    enc_in[0], enc_act[0], enc_out[0] = x0, a0, h1
    received = h1_r
    for t in range(1, half):
        h_in = received
        u = f32(h_in)
        a = bf16(jax.nn.silu(u))
        h_out = bf16(u + conv(a, w_enc))
        enc_in[t], enc_act[t], enc_out[t] = h_in, a, h_out
        if t < half - 1:
            received = up(t, h_out)

    dec_u, dec_act, dec_c = {}, {}, {}
    h_in = enc_out[half - 1]
    u = f32(h_in) + f32(h_in)
    a = bf16(jax.nn.silu(u))
    current = bf16(f32(h_in) + conv(a, w_dec))
    dec_u[half - 1], dec_act[half - 1] = u, a
    for t in range(half - 2, 0, -1):
        h_in = down(t + 1, current)
        u = f32(h_in) + f32(enc_out[t])
        a = bf16(jax.nn.silu(u))
        current = bf16(f32(h_in) + conv(a, w_dec))
        dec_u[t], dec_act[t] = u, a

    u_last = f32(current) + f32(h1_r)
    a_last = bf16(jax.nn.silu(u_last))
    b_last = d_last_r * silu_slope(u_last)
    skip = {1: bf16(b_last)}
    cot = bf16(f32(seed) + b_last)

    for t in range(1, half):
        if t > 1:
            cot = up(t - 1, cot)
        dec_c[t] = cot
        d = conv_t(cot, w_dec)
        b = d * silu_slope(dec_u[t])
        g = bf16(f32(cot) + b)
        if t < half - 1:
            skip[t + 1] = bf16(b)
            cot = g
        else:
            cot = bf16(f32(g) + b)

    enc_c = {}
    for t in range(half - 1, 0, -1):
        if t < half - 1:
            cot = bf16(f32(down(t + 1, cot)) + f32(skip[t + 1]))
        enc_c[t] = cot
        d = conv_t(cot, w_enc)
        b = d * silu_slope(f32(enc_in[t]))
        cot = bf16(f32(cot) + b)
    c0 = bf16(f32(cot) + f32(skip[1]))

    sent = lax.ppermute(jnp.where(lower, c0, a_last), "pipe", [(1, 0), (pipe_size - 2, pipe_size - 1)])
    acts_lo = jnp.stack([a0] + [enc_act[t] for t in range(1, half)])
    cots_lo = jnp.stack([sent] + [enc_c[t] for t in range(1, half)])
    acts_up = jnp.stack([sent] + [dec_act[t] for t in range(1, half)])
    cots_up = jnp.stack([seed] + [dec_c[t] for t in range(1, half)])
    act_sel = jnp.where(lower, acts_lo[stage], acts_up[stage])
    cot_sel = jnp.where(lower, cots_lo[stage], cots_up[stage])
    both = jnp.concatenate([act_sel, cot_sel], axis=-1)
    every = lax.all_gather(both, ("dp", "mp"), axis=0, tiled=True)
    act_all = every[..., :channels]
    cot_all = lax.dynamic_slice_in_dim(every, channels + low, chan_half, 3)
    grad = weight_grad(act_all, cot_all)
    return grad.reshape(1, -1)


def on_stage(active, fn, *args):
    shapes = jax.eval_shape(fn, *args)
    def idle(*unused):
        return jax.tree.map(lambda v: jnp.zeros(v.shape, v.dtype), shapes)
    return lax.cond(active, fn, idle, *args)


def local(latent, section_weight, out_grad):
    pipe_size = lax.axis_size("pipe")
    half = pipe_size // 2
    if half != 2:
        return local_general(latent, section_weight, out_grad)
    device = lax.axis_index("pipe")
    lower = device < half
    stage = jnp.minimum(device, pipe_size - 1 - device)
    lane = lax.axis_index("mp")
    swap = [(0, 1), (1, 0)]

    channels = latent.shape[-1]
    img = latent.shape[-3:]
    samples = latent.reshape((-1,) + img)
    grads = out_grad.reshape((-1,) + img)
    per_lane = samples.shape[0] // 2
    mine = lane * per_lane
    chan_half = section_weight.shape[-1] // (9 * channels)
    low = lane * chan_half

    def take(v, at):
        return lax.dynamic_slice_in_dim(v, at, per_lane, 0)

    own = lax.optimization_barrier(
        section_weight[0].reshape(2, chan_half, 9, channels).transpose(0, 2, 1, 3)
        .reshape(2, 3, 3, chan_half, channels)
    ).transpose(0, 3, 1, 2, 4)

    x0 = take(samples, mine)
    seed = take(grads, mine)
    a0 = bf16(jax.nn.silu(f32(x0)))
    other_enc = lax.ppermute(own[0], "mp", swap)
    other_dec = lax.ppermute(own[1], "mp", swap)

    def join(first, second):
        return jnp.where(lane == 0, jnp.concatenate([first, second], -1),
                         jnp.concatenate([second, first], -1))

    def first(x0, a0, seed, own, other_enc, other_dec):
        h1 = bf16(f32(x0) + join(conv(a0, own[0]), conv(a0, other_enc)))
        high = (1 - lane) * chan_half
        d_own = conv_t(lax.dynamic_slice_in_dim(seed, low, chan_half, 3), own[1])
        d_other = conv_t(lax.dynamic_slice_in_dim(seed, high, chan_half, 3), other_dec)
        return h1, d_own + d_other

    def weights(own, other_enc, other_dec):
        other = jnp.stack([other_enc, other_dec])
        return jnp.where(lane == 0, jnp.concatenate([own, other], 1),
                         jnp.concatenate([other, own], 1))

    h1, d_last = on_stage(stage == 0, first, x0, a0, seed, own, other_enc, other_dec)
    full = on_stage(stage == 1, weights, own, other_enc, other_dec)
    ups = [(0, 1), (pipe_size - 1, pipe_size - 2)]
    h1_r = lax.ppermute(h1, "pipe", ups)
    d_last_r = lax.ppermute(d_last, "pipe", ups)

    def middle(h1_r, d_last_r, seed, full, lower):
        w_enc, w_dec = full[0], full[1]
        u1 = f32(h1_r)
        a1 = bf16(jax.nn.silu(u1))
        h2 = bf16(u1 + conv(a1, w_enc))
        u2 = f32(h2) + f32(h2)
        a2 = bf16(jax.nn.silu(u2))
        h3 = bf16(f32(h2) + conv(a2, w_dec))
        u3 = f32(h3) + u1
        a3 = bf16(jax.nn.silu(u3))
        b3 = d_last_r * silu_slope(u3)
        c2 = bf16(f32(seed) + b3)
        b2 = conv_t(c2, w_dec) * silu_slope(u2)
        g2 = bf16(f32(c2) + b2)
        c1 = bf16(f32(g2) + b2)
        b1 = conv_t(c1, w_enc) * silu_slope(u1)
        g1 = bf16(f32(c1) + b1)
        c0 = bf16(f32(g1) + f32(bf16(b3)))
        return (jnp.where(lower, c0, a3), jnp.where(lower, a1, a2),
                jnp.where(lower, c1, c2))

    back, act1, cot1 = on_stage(stage == 1, middle, h1_r, d_last_r, seed, full, lower)
    sent = lax.ppermute(back, "pipe", [(1, 0), (pipe_size - 2, pipe_size - 1)])

    act_sel = jnp.where(stage == 0, jnp.where(lower, a0, sent), act1)
    cot_sel = jnp.where(stage == 0, jnp.where(lower, sent, seed), cot1)
    both = jnp.concatenate([act_sel, cot_sel], axis=-1)
    every = lax.all_gather(both, ("dp", "mp"), axis=0, tiled=True)
    act_all = every[..., :channels]
    cot_all = lax.dynamic_slice_in_dim(every, channels + low, chan_half, 3)
    grad = weight_grad(act_all, cot_all)
    return grad.reshape(1, -1)


def solution(mesh):
    return jax.shard_map(
        local,
        mesh=mesh,
        in_specs=(
            P(("groups", "dp"), None, None, None, None, None),
            P("pipe", None, "mp"),
            P(("groups", "dp"), None, None, None, None, None),
        ),
        out_specs=P(("groups", "pipe"), "mp"),
        check_vma=False,
    )
```

```python
import jax
import jax.numpy as jnp
from jax import lax
from jax.sharding import PartitionSpec as P


def silu_slope(pre_act):
    sigmoid = jax.nn.sigmoid(pre_act)
    return sigmoid * (1.0 + pre_act * (1.0 - sigmoid))


def conv(act, weight):
    return lax.conv_general_dilated(
        act, weight, (1, 1), ((1, 1), (1, 1)),
        dimension_numbers=("NHWC", "OHWI", "NHWC"),
        preferred_element_type=jnp.float32,
    )


def conv_t(cot, weight):
    flipped = jnp.flip(cot, (1, 2))
    out = lax.conv_general_dilated(
        flipped, weight, (1, 1), ((1, 1), (1, 1)),
        dimension_numbers=("NHWC", "IHWO", "NHWC"),
        preferred_element_type=jnp.float32,
    )
    return jnp.flip(out, (1, 2))


def weight_grad(act, cot):
    return lax.conv_general_dilated(
        act, cot, (1, 1), ((1, 1), (1, 1)),
        dimension_numbers=("CHWN", "IHWO", "CHWN"),
        preferred_element_type=jnp.float32,
    )


def f32(v):
    return v.astype(jnp.float32)


def bf16(v):
    return v.astype(jnp.bfloat16)


def local(latent, section_weight, out_grad):
    pipe_size = lax.axis_size("pipe")
    half = pipe_size // 2
    device = lax.axis_index("pipe")
    lower = device < half
    stage = jnp.minimum(device, pipe_size - 1 - device)
    lane = lax.axis_index("mp")
    swap = [(0, 1), (1, 0)]

    channels = latent.shape[-1]
    img = latent.shape[-3:]
    samples = latent.reshape((-1,) + img)
    grads = out_grad.reshape((-1,) + img)
    per_lane = samples.shape[0] // 2
    mine = lane * per_lane
    theirs = (1 - lane) * per_lane

    chan_half = section_weight.shape[-1] // (9 * channels)
    own = lax.optimization_barrier(
        section_weight[0].reshape(2, chan_half, 9, channels).transpose(0, 2, 1, 3)
        .reshape(2, 3, 3, chan_half, channels)
    ).transpose(0, 3, 1, 2, 4)
    other = lax.ppermute(own, "mp", swap)

    def up(t, v):
        pairs = [(t, t + 1), (pipe_size - 1 - t, pipe_size - 2 - t)]
        return lax.ppermute(v, "pipe", pairs)

    def down(t, v):
        pairs = [(t, t - 1), (pipe_size - 1 - t, pipe_size - t)]
        return lax.ppermute(v, "pipe", pairs)

    def take(v, at):
        return lax.dynamic_slice_in_dim(v, at, per_lane, 0)

    def join(first, second):
        return jnp.where(lane == 0, jnp.concatenate([first, second], -1),
                         jnp.concatenate([second, first], -1))

    low = lane * chan_half
    act_all = bf16(jax.nn.silu(f32(samples)))
    own_in = lax.dynamic_slice_in_dim(samples, low, chan_half, 3)
    h1_half = bf16(f32(own_in) + conv(act_all, own[0]))
    seed_half = lax.dynamic_slice_in_dim(grads, low, chan_half, 3)
    d_part = conv_t(seed_half, own[1])
    parts = lax.all_gather(jnp.concatenate([f32(h1_half), d_part], -1), "mp", axis=0, tiled=False)
    h1 = take(bf16(jnp.concatenate([parts[0, ..., :chan_half], parts[1, ..., :chan_half]], -1)), mine)
    d_last = take(parts[0, ..., chan_half:] + parts[1, ..., chan_half:], mine)
    x0 = take(samples, mine)
    a0 = take(act_all, mine)
    seed = take(grads, mine)
    h1_r = up(0, h1)
    d_last_r = up(0, d_last)

    other, _ = lax.optimization_barrier((other, h1))
    full = jnp.where(lane == 0, jnp.concatenate([own, other], 1),
                     jnp.concatenate([other, own], 1))
    w_enc, w_dec = full[0], full[1]

    enc_in, enc_act, enc_out = {}, {}, {}
    enc_in[0], enc_act[0], enc_out[0] = x0, a0, h1
    received = h1_r
    for t in range(1, half):
        h_in = received
        u = f32(h_in)
        a = bf16(jax.nn.silu(u))
        h_out = bf16(u + conv(a, w_enc))
        enc_in[t], enc_act[t], enc_out[t] = h_in, a, h_out
        if t < half - 1:
            received = up(t, h_out)

    dec_u, dec_act, dec_c = {}, {}, {}
    h_in = enc_out[half - 1]
    u = f32(h_in) + f32(h_in)
    a = bf16(jax.nn.silu(u))
    current = bf16(f32(h_in) + conv(a, w_dec))
    dec_u[half - 1], dec_act[half - 1] = u, a
    for t in range(half - 2, 0, -1):
        h_in = down(t + 1, current)
        u = f32(h_in) + f32(enc_out[t])
        a = bf16(jax.nn.silu(u))
        current = bf16(f32(h_in) + conv(a, w_dec))
        dec_u[t], dec_act[t] = u, a

    u_last = f32(current) + f32(h1_r)
    a_last = bf16(jax.nn.silu(u_last))
    b_last = d_last_r * silu_slope(u_last)
    skip = {1: bf16(b_last)}
    cot = bf16(f32(seed) + b_last)

    for t in range(1, half):
        if t > 1:
            cot = up(t - 1, cot)
        dec_c[t] = cot
        d = conv_t(cot, w_dec)
        b = d * silu_slope(dec_u[t])
        g = bf16(f32(cot) + b)
        if t < half - 1:
            skip[t + 1] = bf16(b)
            cot = g
        else:
            cot = bf16(f32(g) + b)

    enc_c = {}
    for t in range(half - 1, 0, -1):
        if t < half - 1:
            cot = bf16(f32(down(t + 1, cot)) + f32(skip[t + 1]))
        enc_c[t] = cot
        d = conv_t(cot, w_enc)
        b = d * silu_slope(f32(enc_in[t]))
        cot = bf16(f32(cot) + b)
    c0 = bf16(f32(cot) + f32(skip[1]))

    sent = lax.ppermute(jnp.where(lower, c0, a_last), "pipe", [(1, 0), (pipe_size - 2, pipe_size - 1)])
    acts_lo = jnp.stack([a0] + [enc_act[t] for t in range(1, half)])
    cots_lo = jnp.stack([sent] + [enc_c[t] for t in range(1, half)])
    acts_up = jnp.stack([sent] + [dec_act[t] for t in range(1, half)])
    cots_up = jnp.stack([seed] + [dec_c[t] for t in range(1, half)])
    act_sel = jnp.where(lower, acts_lo[stage], acts_up[stage])
    cot_sel = jnp.where(lower, cots_lo[stage], cots_up[stage])
    both = jnp.concatenate([act_sel, cot_sel], axis=-1)
    every = lax.all_gather(both, ("dp", "mp"), axis=0, tiled=True)
    act_all = every[..., :channels]
    cot_all = lax.dynamic_slice_in_dim(every, channels + low, chan_half, 3)
    grad = weight_grad(act_all, cot_all)
    return grad.reshape(1, -1)


def solution(mesh):
    return jax.shard_map(
        local,
        mesh=mesh,
        in_specs=(
            P(("groups", "dp"), None, None, None, None, None),
            P("pipe", None, "mp"),
            P(("groups", "dp"), None, None, None, None, None),
        ),
        out_specs=P(("groups", "pipe"), "mp"),
        check_vma=False,
    )
```

```python
import jax
import jax.numpy as jnp
from jax import lax
from jax.sharding import PartitionSpec as P


def silu_slope(pre_act):
    sigmoid = jax.nn.sigmoid(pre_act)
    return sigmoid * (1.0 + pre_act * (1.0 - sigmoid))


def conv(act, weight):
    return lax.conv_general_dilated(
        act, weight, (1, 1), ((1, 1), (1, 1)),
        dimension_numbers=("NHWC", "OHWI", "NHWC"),
        preferred_element_type=jnp.float32,
    )


def conv_t(cot, weight):
    flipped = jnp.flip(cot, (1, 2))
    out = lax.conv_general_dilated(
        flipped, weight, (1, 1), ((1, 1), (1, 1)),
        dimension_numbers=("NHWC", "IHWO", "NHWC"),
        preferred_element_type=jnp.float32,
    )
    return jnp.flip(out, (1, 2))


def weight_grad(act, cot):
    return lax.conv_general_dilated(
        act, cot, (1, 1), ((1, 1), (1, 1)),
        dimension_numbers=("CHWN", "IHWO", "CHWN"),
        preferred_element_type=jnp.float32,
    )


def f32(v):
    return v.astype(jnp.float32)


def bf16(v):
    return v.astype(jnp.bfloat16)


def local(latent, section_weight, out_grad):
    pipe_size = lax.axis_size("pipe")
    half = pipe_size // 2
    device = lax.axis_index("pipe")
    lower = device < half
    stage = jnp.minimum(device, pipe_size - 1 - device)
    lane = lax.axis_index("mp")
    swap = [(0, 1), (1, 0)]

    channels = latent.shape[-1]
    img = latent.shape[-3:]
    samples = latent.reshape((-1,) + img)
    grads = out_grad.reshape((-1,) + img)
    per_lane = samples.shape[0] // 2
    mine = lane * per_lane
    theirs = (1 - lane) * per_lane

    chan_half = section_weight.shape[-1] // (9 * channels)
    own = lax.optimization_barrier(
        section_weight[0].reshape(2, chan_half, 9, channels).transpose(0, 2, 1, 3)
        .reshape(2, 3, 3, chan_half, channels)
    ).transpose(0, 3, 1, 2, 4)
    other = lax.ppermute(own, "mp", swap)

    def up(t, v):
        pairs = [(t, t + 1), (pipe_size - 1 - t, pipe_size - 2 - t)]
        return lax.ppermute(v, "pipe", pairs)

    def down(t, v):
        pairs = [(t, t - 1), (pipe_size - 1 - t, pipe_size - t)]
        return lax.ppermute(v, "pipe", pairs)

    def take(v, at):
        return lax.dynamic_slice_in_dim(v, at, per_lane, 0)

    def join(first, second):
        return jnp.where(lane == 0, jnp.concatenate([first, second], -1),
                         jnp.concatenate([second, first], -1))

    low = lane * chan_half
    act_all = bf16(jax.nn.silu(f32(samples)))
    own_in = lax.dynamic_slice_in_dim(samples, low, chan_half, 3)
    h1_half = bf16(f32(own_in) + conv(act_all, own[0]))
    seed_half = lax.dynamic_slice_in_dim(grads, low, chan_half, 3)
    d_part = conv_t(seed_half, own[1])
    parts = lax.all_gather(jnp.concatenate([f32(h1_half), d_part], -1), "mp", axis=0, tiled=False)
    h1 = take(bf16(jnp.concatenate([parts[0, ..., :chan_half], parts[1, ..., :chan_half]], -1)), mine)
    d_last = take(parts[0, ..., chan_half:] + parts[1, ..., chan_half:], mine)
    x0 = take(samples, mine)
    a0 = take(act_all, mine)
    seed = take(grads, mine)
    h1_r = up(0, h1)
    d_last_r = up(0, d_last)

    def assemble(mine_half, their_half):
        return jnp.where(lane == 0, jnp.concatenate([mine_half, their_half], 0),
                         jnp.concatenate([their_half, mine_half], 0))

    other_enc, _ = lax.optimization_barrier((other[0], h1))
    w_enc = assemble(own[0], other_enc)

    enc_in, enc_act, enc_out = {}, {}, {}
    enc_in[0], enc_act[0], enc_out[0] = x0, a0, h1
    received = h1_r
    for t in range(1, half):
        h_in = received
        u = f32(h_in)
        a = bf16(jax.nn.silu(u))
        h_out = bf16(u + conv(a, w_enc))
        enc_in[t], enc_act[t], enc_out[t] = h_in, a, h_out
        if t < half - 1:
            received = up(t, h_out)

    dec_u, dec_act, dec_c = {}, {}, {}
    other_dec, h_in = lax.optimization_barrier((other[1], enc_out[half - 1]))
    w_dec = assemble(own[1], other_dec)
    u = f32(h_in) + f32(h_in)
    a = bf16(jax.nn.silu(u))
    current = bf16(f32(h_in) + conv(a, w_dec))
    dec_u[half - 1], dec_act[half - 1] = u, a
    for t in range(half - 2, 0, -1):
        h_in = down(t + 1, current)
        u = f32(h_in) + f32(enc_out[t])
        a = bf16(jax.nn.silu(u))
        current = bf16(f32(h_in) + conv(a, w_dec))
        dec_u[t], dec_act[t] = u, a

    u_last = f32(current) + f32(h1_r)
    a_last = bf16(jax.nn.silu(u_last))
    b_last = d_last_r * silu_slope(u_last)
    skip = {1: bf16(b_last)}
    cot = bf16(f32(seed) + b_last)

    for t in range(1, half):
        if t > 1:
            cot = up(t - 1, cot)
        dec_c[t] = cot
        d = conv_t(cot, w_dec)
        b = d * silu_slope(dec_u[t])
        g = bf16(f32(cot) + b)
        if t < half - 1:
            skip[t + 1] = bf16(b)
            cot = g
        else:
            cot = bf16(f32(g) + b)

    enc_c = {}
    for t in range(half - 1, 0, -1):
        if t < half - 1:
            cot = bf16(f32(down(t + 1, cot)) + f32(skip[t + 1]))
        enc_c[t] = cot
        d = conv_t(cot, w_enc)
        b = d * silu_slope(f32(enc_in[t]))
        cot = bf16(f32(cot) + b)
    c0 = bf16(f32(cot) + f32(skip[1]))

    sent = lax.ppermute(jnp.where(lower, c0, a_last), "pipe", [(1, 0), (pipe_size - 2, pipe_size - 1)])
    acts_lo = jnp.stack([a0] + [enc_act[t] for t in range(1, half)])
    cots_lo = jnp.stack([sent] + [enc_c[t] for t in range(1, half)])
    acts_up = jnp.stack([sent] + [dec_act[t] for t in range(1, half)])
    cots_up = jnp.stack([seed] + [dec_c[t] for t in range(1, half)])
    act_sel = jnp.where(lower, acts_lo[stage], acts_up[stage])
    cot_sel = jnp.where(lower, cots_lo[stage], cots_up[stage])
    both = jnp.concatenate([act_sel, cot_sel], axis=-1)
    every = lax.all_gather(both, ("dp", "mp"), axis=0, tiled=True)
    act_all = every[..., :channels]
    cot_all = lax.dynamic_slice_in_dim(every, channels + low, chan_half, 3)
    grad = weight_grad(act_all, cot_all)
    return grad.reshape(1, -1)


def solution(mesh):
    return jax.shard_map(
        local,
        mesh=mesh,
        in_specs=(
            P(("groups", "dp"), None, None, None, None, None),
            P("pipe", None, "mp"),
            P(("groups", "dp"), None, None, None, None, None),
        ),
        out_specs=P(("groups", "pipe"), "mp"),
        check_vma=False,
    )
```

```python
import jax
import jax.numpy as jnp
from jax import lax
from jax.sharding import PartitionSpec as P


def silu_slope(pre_act):
    sigmoid = jax.nn.sigmoid(pre_act)
    return sigmoid * (1.0 + pre_act * (1.0 - sigmoid))


def conv(act, weight):
    return lax.conv_general_dilated(
        act, weight, (1, 1), ((1, 1), (1, 1)),
        dimension_numbers=("NHWC", "OHWI", "NHWC"),
        preferred_element_type=jnp.float32,
    )


def conv_t(cot, weight):
    flipped = jnp.flip(cot, (1, 2))
    out = lax.conv_general_dilated(
        flipped, weight, (1, 1), ((1, 1), (1, 1)),
        dimension_numbers=("NHWC", "IHWO", "NHWC"),
        preferred_element_type=jnp.float32,
    )
    return jnp.flip(out, (1, 2))


def weight_grad(act, cot):
    return lax.conv_general_dilated(
        act, cot, (1, 1), ((1, 1), (1, 1)),
        dimension_numbers=("CHWN", "IHWO", "CHWN"),
        preferred_element_type=jnp.float32,
    )


def f32(v):
    return v.astype(jnp.float32)


def bf16(v):
    return v.astype(jnp.bfloat16)


def local(latent, section_weight, out_grad):
    pipe_size = lax.axis_size("pipe")
    half = pipe_size // 2
    device = lax.axis_index("pipe")
    lower = device < half
    stage = jnp.minimum(device, pipe_size - 1 - device)
    lane = lax.axis_index("mp")
    swap = [(0, 1), (1, 0)]

    channels = latent.shape[-1]
    img = latent.shape[-3:]
    samples = latent.reshape((-1,) + img)
    grads = out_grad.reshape((-1,) + img)
    per_lane = samples.shape[0] // 2
    mine = lane * per_lane
    theirs = (1 - lane) * per_lane

    chan_half = section_weight.shape[-1] // (9 * channels)
    own = lax.optimization_barrier(
        section_weight[0].reshape(2, chan_half, 9, channels).transpose(0, 2, 1, 3)
        .reshape(2, 3, 3, chan_half, channels)
    ).transpose(0, 3, 1, 2, 4)
    other = lax.ppermute(own, "mp", swap)

    def up(t, v):
        pairs = [(t, t + 1), (pipe_size - 1 - t, pipe_size - 2 - t)]
        return lax.ppermute(v, "pipe", pairs)

    def down(t, v):
        pairs = [(t, t - 1), (pipe_size - 1 - t, pipe_size - t)]
        return lax.ppermute(v, "pipe", pairs)

    def take(v, at):
        return lax.dynamic_slice_in_dim(v, at, per_lane, 0)

    def join(first, second):
        return jnp.where(lane == 0, jnp.concatenate([first, second], -1),
                         jnp.concatenate([second, first], -1))

    low = lane * chan_half
    act_all = bf16(jax.nn.silu(f32(samples)))
    own_in = lax.dynamic_slice_in_dim(samples, low, chan_half, 3)
    h1_half = bf16(f32(own_in) + conv(act_all, own[0]))
    seed_half = lax.dynamic_slice_in_dim(grads, low, chan_half, 3)
    d_part = conv_t(seed_half, own[1])
    parts = lax.all_gather(jnp.concatenate([f32(h1_half), d_part], -1), "mp", axis=0, tiled=False)
    h1 = take(bf16(jnp.concatenate([parts[0, ..., :chan_half], parts[1, ..., :chan_half]], -1)), mine)
    d_last = take(parts[0, ..., chan_half:] + parts[1, ..., chan_half:], mine)
    x0 = take(samples, mine)
    a0 = take(act_all, mine)
    seed = take(grads, mine)
    h1_r = up(0, h1)
    d_last_r = up(0, d_last)

    other, _ = lax.optimization_barrier((other, h1))
    full = jnp.where(lane == 0, jnp.concatenate([own, other], 1),
                     jnp.concatenate([other, own], 1))
    w_enc, w_dec = full[0], full[1]

    enc_in, enc_act, enc_out = {}, {}, {}
    enc_in[0], enc_act[0], enc_out[0] = x0, a0, h1
    received = h1_r
    for t in range(1, half):
        h_in = received
        u = f32(h_in)
        a = bf16(jax.nn.silu(u))
        h_out = bf16(u + conv(a, w_enc))
        enc_in[t], enc_act[t], enc_out[t] = h_in, a, h_out
        if t < half - 1:
            received = up(t, h_out)

    dec_u, dec_act, dec_c = {}, {}, {}
    h_in = enc_out[half - 1]
    u = f32(h_in) + f32(h_in)
    a = bf16(jax.nn.silu(u))
    current = bf16(f32(h_in) + conv(a, w_dec))
    dec_u[half - 1], dec_act[half - 1] = u, a
    for t in range(half - 2, 0, -1):
        h_in = down(t + 1, current)
        u = f32(h_in) + f32(enc_out[t])
        a = bf16(jax.nn.silu(u))
        current = bf16(f32(h_in) + conv(a, w_dec))
        dec_u[t], dec_act[t] = u, a

    u_last = f32(current) + f32(h1_r)
    a_last = bf16(jax.nn.silu(u_last))
    b_last = d_last_r * silu_slope(u_last)
    skip = {1: bf16(b_last)}
    cot = bf16(f32(seed) + b_last)

    for t in range(1, half):
        if t > 1:
            cot = up(t - 1, cot)
        dec_c[t] = cot
        d = conv_t(cot, w_dec)
        b = d * silu_slope(dec_u[t])
        g = bf16(f32(cot) + b)
        if t < half - 1:
            skip[t + 1] = bf16(b)
            cot = g
        else:
            cot = bf16(f32(g) + b)

    enc_c = {}
    for t in range(half - 1, 0, -1):
        if t < half - 1:
            cot = bf16(f32(down(t + 1, cot)) + f32(skip[t + 1]))
        enc_c[t] = cot
        d = conv_t(cot, w_enc)
        b = d * silu_slope(f32(enc_in[t]))
        cot = bf16(f32(cot) + b)
    c0 = bf16(f32(cot) + f32(skip[1]))

    sent = lax.ppermute(jnp.where(lower, c0, a_last), "pipe", [(1, 0), (pipe_size - 2, pipe_size - 1)])
    acts_lo = jnp.stack([a0] + [enc_act[t] for t in range(1, half)])
    cots_lo = jnp.stack([sent] + [enc_c[t] for t in range(1, half)])
    acts_up = jnp.stack([sent] + [dec_act[t] for t in range(1, half)])
    cots_up = jnp.stack([seed] + [dec_c[t] for t in range(1, half)])
    act_sel = jnp.where(lower, acts_lo[stage], acts_up[stage])
    cot_sel = jnp.where(lower, cots_lo[stage], cots_up[stage])
    swapped = (stage == 0) & jnp.logical_not(lower)
    early = jnp.where(swapped, cot_sel, act_sel)
    late = jnp.where(swapped, act_sel, cot_sel)
    early, _ = lax.optimization_barrier((early, c0))
    early_all = lax.all_gather(early, ("dp", "mp"), axis=0, tiled=True)
    late, _ = lax.optimization_barrier((late, early_all))
    late_all = lax.all_gather(late, ("dp", "mp"), axis=0, tiled=True)
    act_all = jnp.where(swapped, late_all, early_all)
    cot_all = lax.dynamic_slice_in_dim(jnp.where(swapped, early_all, late_all), low, chan_half, 3)
    grad = weight_grad(act_all, cot_all)
    return grad.reshape(1, -1)


def solution(mesh):
    return jax.shard_map(
        local,
        mesh=mesh,
        in_specs=(
            P(("groups", "dp"), None, None, None, None, None),
            P("pipe", None, "mp"),
            P(("groups", "dp"), None, None, None, None, None),
        ),
        out_specs=P(("groups", "pipe"), "mp"),
        check_vma=False,
    )
```

```python
import jax
import jax.numpy as jnp
from jax import lax
from jax.sharding import PartitionSpec as P


def silu_slope(pre_act):
    sigmoid = jax.nn.sigmoid(pre_act)
    return sigmoid * (1.0 + pre_act * (1.0 - sigmoid))


def conv(act, weight):
    return lax.conv_general_dilated(
        act, weight, (1, 1), ((1, 1), (1, 1)),
        dimension_numbers=("NHWC", "OHWI", "NHWC"),
        preferred_element_type=jnp.float32,
    )


def conv_t(cot, weight):
    flipped = jnp.flip(cot, (1, 2))
    out = lax.conv_general_dilated(
        flipped, weight, (1, 1), ((1, 1), (1, 1)),
        dimension_numbers=("NHWC", "IHWO", "NHWC"),
        preferred_element_type=jnp.float32,
    )
    return jnp.flip(out, (1, 2))


def weight_grad(act, cot):
    return lax.conv_general_dilated(
        act, cot, (1, 1), ((1, 1), (1, 1)),
        dimension_numbers=("CHWN", "IHWO", "CHWN"),
        preferred_element_type=jnp.float32,
    )


def f32(v):
    return v.astype(jnp.float32)


def bf16(v):
    return v.astype(jnp.bfloat16)


def local(latent, section_weight, out_grad):
    pipe_size = lax.axis_size("pipe")
    half = pipe_size // 2
    device = lax.axis_index("pipe")
    lower = device < half
    stage = jnp.minimum(device, pipe_size - 1 - device)
    lane = lax.axis_index("mp")
    swap = [(0, 1), (1, 0)]

    channels = latent.shape[-1]
    img = latent.shape[-3:]
    samples = latent.reshape((-1,) + img)
    grads = out_grad.reshape((-1,) + img)
    per_lane = samples.shape[0] // 2
    mine = lane * per_lane
    theirs = (1 - lane) * per_lane

    chan_half = section_weight.shape[-1] // (9 * channels)
    own = lax.optimization_barrier(
        section_weight[0].reshape(2, chan_half, 9, channels).transpose(0, 2, 1, 3)
        .reshape(2, 3, 3, chan_half, channels)
    ).transpose(0, 3, 1, 2, 4)
    other = lax.ppermute(own, "mp", swap)

    def up(t, v):
        pairs = [(t, t + 1), (pipe_size - 1 - t, pipe_size - 2 - t)]
        return lax.ppermute(v, "pipe", pairs)

    def down(t, v):
        pairs = [(t, t - 1), (pipe_size - 1 - t, pipe_size - t)]
        return lax.ppermute(v, "pipe", pairs)

    def take(v, at):
        return lax.dynamic_slice_in_dim(v, at, per_lane, 0)

    def join(first, second):
        return jnp.where(lane == 0, jnp.concatenate([first, second], -1),
                         jnp.concatenate([second, first], -1))

    low = lane * chan_half
    act_all = bf16(jax.nn.silu(f32(samples)))
    own_in = lax.dynamic_slice_in_dim(samples, low, chan_half, 3)
    h1_half = bf16(f32(own_in) + conv(act_all, own[0]))
    seed_half = lax.dynamic_slice_in_dim(grads, low, chan_half, 3)
    d_part = conv_t(seed_half, own[1])
    parts = lax.all_gather(jnp.concatenate([f32(h1_half), d_part], -1), "mp", axis=0, tiled=False)
    h1 = take(bf16(jnp.concatenate([parts[0, ..., :chan_half], parts[1, ..., :chan_half]], -1)), mine)
    d_last = take(parts[0, ..., chan_half:] + parts[1, ..., chan_half:], mine)
    x0 = take(samples, mine)
    a0 = take(act_all, mine)
    seed = take(grads, mine)
    h1_r = up(0, h1)
    d_last_r = up(0, d_last)

    other, _ = lax.optimization_barrier((other, h1))
    full = jnp.where(lane == 0, jnp.concatenate([own, other], 1),
                     jnp.concatenate([other, own], 1))
    w_enc, w_dec = full[0], full[1]

    enc_in, enc_act, enc_out = {}, {}, {}
    enc_in[0], enc_act[0], enc_out[0] = x0, a0, h1
    received = h1_r
    for t in range(1, half):
        h_in = received
        u = f32(h_in)
        a = bf16(jax.nn.silu(u))
        h_out = bf16(u + conv(a, w_enc))
        enc_in[t], enc_act[t], enc_out[t] = h_in, a, h_out
        if t < half - 1:
            received = up(t, h_out)

    dec_u, dec_act, dec_c = {}, {}, {}
    h_in = enc_out[half - 1]
    u = f32(h_in) + f32(h_in)
    a = bf16(jax.nn.silu(u))
    current = bf16(f32(h_in) + conv(a, w_dec))
    dec_u[half - 1], dec_act[half - 1] = u, a
    for t in range(half - 2, 0, -1):
        h_in = down(t + 1, current)
        u = f32(h_in) + f32(enc_out[t])
        a = bf16(jax.nn.silu(u))
        current = bf16(f32(h_in) + conv(a, w_dec))
        dec_u[t], dec_act[t] = u, a

    u_last = f32(current) + f32(h1_r)
    a_last = bf16(jax.nn.silu(u_last))
    b_last = d_last_r * silu_slope(u_last)
    skip = {1: bf16(b_last)}
    cot = bf16(f32(seed) + b_last)

    for t in range(1, half):
        if t > 1:
            cot = up(t - 1, cot)
        dec_c[t] = cot
        d = conv_t(cot, w_dec)
        b = d * silu_slope(dec_u[t])
        g = bf16(f32(cot) + b)
        if t < half - 1:
            skip[t + 1] = bf16(b)
            cot = g
        else:
            cot = bf16(f32(g) + b)

    enc_c = {}
    for t in range(half - 1, 0, -1):
        if t < half - 1:
            cot = bf16(f32(down(t + 1, cot)) + f32(skip[t + 1]))
        enc_c[t] = cot
        d = conv_t(cot, w_enc)
        b = d * silu_slope(f32(enc_in[t]))
        cot = bf16(f32(cot) + b)
    c0 = bf16(f32(cot) + f32(skip[1]))

    nd = lax.axis_size("dp")
    pair0, _ = lax.optimization_barrier((jnp.concatenate([x0, seed], -1), h1_r))
    others = [pair0] + [lax.ppermute(pair0, "dp", [((d + dd) % nd, d) for d in range(nd)])
                        for dd in range(1, nd)]
    back = jnp.where(lower, c0, a_last)

    def to_first(dd):
        pairs = [(src * nd + (d + dd) % nd, dst * nd + d)
                 for src, dst in ((1, 0), (pipe_size - 2, pipe_size - 1)) for d in range(nd)]
        return lax.ppermute(back, ("pipe", "dp"), pairs)

    acts_lo = jnp.stack([enc_act[t] for t in range(1, half)])
    cots_lo = jnp.stack([enc_c[t] for t in range(1, half)])
    acts_up = jnp.stack([dec_act[t] for t in range(1, half)])
    cots_up = jnp.stack([dec_c[t] for t in range(1, half)])
    at = jnp.maximum(stage - 1, 0)
    own_pair = jnp.concatenate([jnp.where(lower, acts_lo[at], acts_up[at]),
                                jnp.where(lower, cots_lo[at], cots_up[at])], -1)
    inner = [j for j in range(pipe_size) if min(j, pipe_size - 1 - j) >= 1]

    def among(dd):
        pairs = [(j * nd + (d + dd) % nd, j * nd + d) for j in inner for d in range(nd)]
        return lax.ppermute(own_pair, ("pipe", "dp"), pairs)

    got = [to_first(dd) for dd in range(nd)]
    mids = [own_pair] + [among(dd) for dd in range(1, nd)]
    pieces = []
    for dd in range(nd):
        a_first = bf16(jax.nn.silu(f32(others[dd][..., :channels])))
        act = jnp.where(lower, a_first, got[dd])
        cot = jnp.where(lower, got[dd], others[dd][..., channels:])
        first_pair = jnp.concatenate([act, cot], -1)
        pieces.append(jnp.where(stage == 0, first_pair, mids[dd]))
    every = lax.all_gather(jnp.concatenate(pieces, 0), "mp", axis=0, tiled=True)
    act_all = every[..., :channels]
    cot_all = lax.dynamic_slice_in_dim(every, channels + low, chan_half, 3)
    grad = weight_grad(act_all, cot_all)
    return grad.reshape(1, -1)


def solution(mesh):
    return jax.shard_map(
        local,
        mesh=mesh,
        in_specs=(
            P(("groups", "dp"), None, None, None, None, None),
            P("pipe", None, "mp"),
            P(("groups", "dp"), None, None, None, None, None),
        ),
        out_specs=P(("groups", "pipe"), "mp"),
        check_vma=False,
    )
```

```python
import jax
import jax.numpy as jnp
from jax import lax
from jax.sharding import PartitionSpec as P


def silu_slope(pre_act):
    sigmoid = jax.nn.sigmoid(pre_act)
    return sigmoid * (1.0 + pre_act * (1.0 - sigmoid))


def conv(act, weight):
    return lax.conv_general_dilated(
        act, weight, (1, 1), ((1, 1), (1, 1)),
        dimension_numbers=("NHWC", "OHWI", "NHWC"),
        preferred_element_type=jnp.float32,
    )


def conv_t(cot, weight):
    flipped = jnp.flip(cot, (1, 2))
    out = lax.conv_general_dilated(
        flipped, weight, (1, 1), ((1, 1), (1, 1)),
        dimension_numbers=("NHWC", "IHWO", "NHWC"),
        preferred_element_type=jnp.float32,
    )
    return jnp.flip(out, (1, 2))


def weight_grad(act, cot):
    return lax.conv_general_dilated(
        act, cot, (1, 1), ((1, 1), (1, 1)),
        dimension_numbers=("CHWN", "IHWO", "CHWN"),
        preferred_element_type=jnp.float32,
    )


def f32(v):
    return v.astype(jnp.float32)


def bf16(v):
    return v.astype(jnp.bfloat16)


def local(latent, section_weight, out_grad):
    pipe_size = lax.axis_size("pipe")
    half = pipe_size // 2
    device = lax.axis_index("pipe")
    lower = device < half
    stage = jnp.minimum(device, pipe_size - 1 - device)
    lane = lax.axis_index("mp")
    swap = [(0, 1), (1, 0)]

    channels = latent.shape[-1]
    img = latent.shape[-3:]
    samples = latent.reshape((-1,) + img)
    grads = out_grad.reshape((-1,) + img)
    per_lane = samples.shape[0] // 2
    mine = lane * per_lane
    theirs = (1 - lane) * per_lane

    chan_half = section_weight.shape[-1] // (9 * channels)
    own = lax.optimization_barrier(
        section_weight[0].reshape(2, chan_half, 9, channels).transpose(0, 2, 1, 3)
        .reshape(2, 3, 3, chan_half, channels)
    ).transpose(0, 3, 1, 2, 4)
    other = lax.ppermute(own, "mp", swap)

    def up(t, v):
        pairs = [(t, t + 1), (pipe_size - 1 - t, pipe_size - 2 - t)]
        return lax.ppermute(v, "pipe", pairs)

    def down(t, v):
        pairs = [(t, t - 1), (pipe_size - 1 - t, pipe_size - t)]
        return lax.ppermute(v, "pipe", pairs)

    def take(v, at):
        return lax.dynamic_slice_in_dim(v, at, per_lane, 0)

    def join(first, second):
        return jnp.where(lane == 0, jnp.concatenate([first, second], -1),
                         jnp.concatenate([second, first], -1))

    low = lane * chan_half
    act_all = bf16(jax.nn.silu(f32(samples)))
    own_in = lax.dynamic_slice_in_dim(samples, low, chan_half, 3)
    h1_half = bf16(f32(own_in) + conv(act_all, own[0]))
    seed_half = lax.dynamic_slice_in_dim(grads, low, chan_half, 3)
    d_part = conv_t(seed_half, own[1])
    parts = lax.all_gather(jnp.concatenate([f32(h1_half), d_part], -1), "mp", axis=0, tiled=False)
    h1 = take(bf16(jnp.concatenate([parts[0, ..., :chan_half], parts[1, ..., :chan_half]], -1)), mine)
    d_last = take(parts[0, ..., chan_half:] + parts[1, ..., chan_half:], mine)
    x0 = take(samples, mine)
    a0 = take(act_all, mine)
    seed = take(grads, mine)
    h1_r = up(0, h1)
    d_last_r = up(0, d_last)

    other, _ = lax.optimization_barrier((other, h1))
    full = jnp.where(lane == 0, jnp.concatenate([own, other], 1),
                     jnp.concatenate([other, own], 1))
    w_enc, w_dec = full[0], full[1]

    enc_in, enc_act, enc_out = {}, {}, {}
    enc_in[0], enc_act[0], enc_out[0] = x0, a0, h1
    received = h1_r
    for t in range(1, half):
        h_in = received
        u = f32(h_in)
        a = bf16(jax.nn.silu(u))
        h_out = bf16(u + conv(a, w_enc))
        enc_in[t], enc_act[t], enc_out[t] = h_in, a, h_out
        if t < half - 1:
            received = up(t, h_out)

    dec_u, dec_act, dec_c = {}, {}, {}
    h_in = enc_out[half - 1]
    u = f32(h_in) + f32(h_in)
    a = bf16(jax.nn.silu(u))
    current = bf16(f32(h_in) + conv(a, w_dec))
    dec_u[half - 1], dec_act[half - 1] = u, a
    for t in range(half - 2, 0, -1):
        h_in = down(t + 1, current)
        u = f32(h_in) + f32(enc_out[t])
        a = bf16(jax.nn.silu(u))
        current = bf16(f32(h_in) + conv(a, w_dec))
        dec_u[t], dec_act[t] = u, a

    u_last = f32(current) + f32(h1_r)
    a_last = bf16(jax.nn.silu(u_last))
    b_last = d_last_r * silu_slope(u_last)
    skip = {1: bf16(b_last)}
    cot = bf16(f32(seed) + b_last)

    for t in range(1, half):
        if t > 1:
            cot = up(t - 1, cot)
        dec_c[t] = cot
        d = conv_t(cot, w_dec)
        b = d * silu_slope(dec_u[t])
        g = bf16(f32(cot) + b)
        if t < half - 1:
            skip[t + 1] = bf16(b)
            cot = g
        else:
            cot = bf16(f32(g) + b)

    enc_c = {}
    for t in range(half - 1, 0, -1):
        if t < half - 1:
            cot = bf16(f32(down(t + 1, cot)) + f32(skip[t + 1]))
        enc_c[t] = cot
        d = conv_t(cot, w_enc)
        b = d * silu_slope(f32(enc_in[t]))
        cot = bf16(f32(cot) + b)
    c0 = bf16(f32(cot) + f32(skip[1]))

    nd = lax.axis_size("dp")
    back = jnp.where(lower, jnp.concatenate([a0, c0], -1), jnp.concatenate([a_last, seed], -1))

    def to_first(dd):
        pairs = [(src * nd + (d + dd) % nd, dst * nd + d)
                 for src, dst in ((1, 0), (pipe_size - 2, pipe_size - 1)) for d in range(nd)]
        return lax.ppermute(back, ("pipe", "dp"), pairs)

    acts_lo = jnp.stack([enc_act[t] for t in range(1, half)])
    cots_lo = jnp.stack([enc_c[t] for t in range(1, half)])
    acts_up = jnp.stack([dec_act[t] for t in range(1, half)])
    cots_up = jnp.stack([dec_c[t] for t in range(1, half)])
    at = jnp.maximum(stage - 1, 0)
    own_pair = jnp.concatenate([jnp.where(lower, acts_lo[at], acts_up[at]),
                                jnp.where(lower, cots_lo[at], cots_up[at])], -1)
    inner = [j for j in range(pipe_size) if min(j, pipe_size - 1 - j) >= 1]

    def among(dd):
        pairs = [(j * nd + (d + dd) % nd, j * nd + d) for j in inner for d in range(nd)]
        return lax.ppermute(own_pair, ("pipe", "dp"), pairs)

    got = [to_first(dd) for dd in range(nd)]
    mids = [own_pair] + [among(dd) for dd in range(1, nd)]
    pieces = [jnp.where(stage == 0, got[dd], mids[dd]) for dd in range(nd)]
    every = lax.all_gather(jnp.concatenate(pieces, 0), "mp", axis=0, tiled=True)
    act_all = every[..., :channels]
    cot_all = lax.dynamic_slice_in_dim(every, channels + low, chan_half, 3)
    grad = weight_grad(act_all, cot_all)
    return grad.reshape(1, -1)


def solution(mesh):
    return jax.shard_map(
        local,
        mesh=mesh,
        in_specs=(
            P(("groups", "dp"), None, None, None, None, None),
            P("pipe", None, "mp"),
            P(("groups", "dp"), None, None, None, None, None),
        ),
        out_specs=P(("groups", "pipe"), "mp"),
        check_vma=False,
    )
```

```python
import jax
import jax.numpy as jnp
from jax import lax
from jax.sharding import PartitionSpec as P


def silu_slope(pre_act):
    sigmoid = jax.nn.sigmoid(pre_act)
    return sigmoid * (1.0 + pre_act * (1.0 - sigmoid))


def conv(act, weight):
    return lax.conv_general_dilated(
        act, weight, (1, 1), ((1, 1), (1, 1)),
        dimension_numbers=("NHWC", "OHWI", "NHWC"),
        preferred_element_type=jnp.float32,
    )


def conv_t(cot, weight):
    flipped = jnp.flip(cot, (1, 2))
    out = lax.conv_general_dilated(
        flipped, weight, (1, 1), ((1, 1), (1, 1)),
        dimension_numbers=("NHWC", "IHWO", "NHWC"),
        preferred_element_type=jnp.float32,
    )
    return jnp.flip(out, (1, 2))


def weight_grad(act, cot):
    return lax.conv_general_dilated(
        act, cot, (1, 1), ((1, 1), (1, 1)),
        dimension_numbers=("CHWN", "IHWO", "CHWN"),
        preferred_element_type=jnp.float32,
    )


def f32(v):
    return v.astype(jnp.float32)


def bf16(v):
    return v.astype(jnp.bfloat16)


def local(latent, section_weight, out_grad):
    pipe_size = lax.axis_size("pipe")
    half = pipe_size // 2
    device = lax.axis_index("pipe")
    lower = device < half
    stage = jnp.minimum(device, pipe_size - 1 - device)
    lane = lax.axis_index("mp")
    swap = [(0, 1), (1, 0)]

    channels = latent.shape[-1]
    img = latent.shape[-3:]
    samples = latent.reshape((-1,) + img)
    grads = out_grad.reshape((-1,) + img)
    per_lane = samples.shape[0] // 2
    mine = lane * per_lane
    theirs = (1 - lane) * per_lane

    chan_half = section_weight.shape[-1] // (9 * channels)
    own = lax.optimization_barrier(
        section_weight[0].reshape(2, chan_half, 9, channels).transpose(0, 2, 1, 3)
        .reshape(2, 3, 3, chan_half, channels)
    ).transpose(0, 3, 1, 2, 4)
    other = lax.ppermute(own, "mp", swap)

    def up(t, v):
        pairs = [(t, t + 1), (pipe_size - 1 - t, pipe_size - 2 - t)]
        return lax.ppermute(v, "pipe", pairs)

    def down(t, v):
        pairs = [(t, t - 1), (pipe_size - 1 - t, pipe_size - t)]
        return lax.ppermute(v, "pipe", pairs)

    def take(v, at):
        return lax.dynamic_slice_in_dim(v, at, per_lane, 0)

    def join(first, second):
        return jnp.where(lane == 0, jnp.concatenate([first, second], -1),
                         jnp.concatenate([second, first], -1))

    low = lane * chan_half
    act_all = bf16(jax.nn.silu(f32(samples)))
    own_in = lax.dynamic_slice_in_dim(samples, low, chan_half, 3)
    h1_half = bf16(f32(own_in) + conv(act_all, own[0]))
    seed_half = lax.dynamic_slice_in_dim(grads, low, chan_half, 3)
    d_part = conv_t(seed_half, own[1])
    parts = lax.all_gather(jnp.concatenate([f32(h1_half), d_part], -1), "mp", axis=0, tiled=False)
    h1 = take(bf16(jnp.concatenate([parts[0, ..., :chan_half], parts[1, ..., :chan_half]], -1)), mine)
    d_last = take(parts[0, ..., chan_half:] + parts[1, ..., chan_half:], mine)
    x0 = take(samples, mine)
    a0 = take(act_all, mine)
    seed = take(grads, mine)
    other, h1 = lax.optimization_barrier((other, h1))
    h1_r = up(0, h1)
    d_last_r = up(0, d_last)

    full = jnp.where(lane == 0, jnp.concatenate([own, other], 1),
                     jnp.concatenate([other, own], 1))
    w_enc, w_dec = full[0], full[1]

    enc_in, enc_act, enc_out = {}, {}, {}
    enc_in[0], enc_act[0], enc_out[0] = x0, a0, h1
    received = h1_r
    for t in range(1, half):
        h_in = received
        u = f32(h_in)
        a = bf16(jax.nn.silu(u))
        h_out = bf16(u + conv(a, w_enc))
        enc_in[t], enc_act[t], enc_out[t] = h_in, a, h_out
        if t < half - 1:
            received = up(t, h_out)

    dec_u, dec_act, dec_c = {}, {}, {}
    h_in = enc_out[half - 1]
    u = f32(h_in) + f32(h_in)
    a = bf16(jax.nn.silu(u))
    current = bf16(f32(h_in) + conv(a, w_dec))
    dec_u[half - 1], dec_act[half - 1] = u, a
    for t in range(half - 2, 0, -1):
        h_in = down(t + 1, current)
        u = f32(h_in) + f32(enc_out[t])
        a = bf16(jax.nn.silu(u))
        current = bf16(f32(h_in) + conv(a, w_dec))
        dec_u[t], dec_act[t] = u, a

    u_last = f32(current) + f32(h1_r)
    a_last = bf16(jax.nn.silu(u_last))
    b_last = d_last_r * silu_slope(u_last)
    skip = {1: bf16(b_last)}
    cot = bf16(f32(seed) + b_last)

    for t in range(1, half):
        if t > 1:
            cot = up(t - 1, cot)
        dec_c[t] = cot
        d = conv_t(cot, w_dec)
        b = d * silu_slope(dec_u[t])
        g = bf16(f32(cot) + b)
        if t < half - 1:
            skip[t + 1] = bf16(b)
            cot = g
        else:
            cot = bf16(f32(g) + b)

    enc_c = {}
    for t in range(half - 1, 0, -1):
        if t < half - 1:
            cot = bf16(f32(down(t + 1, cot)) + f32(skip[t + 1]))
        enc_c[t] = cot
        d = conv_t(cot, w_enc)
        b = d * silu_slope(f32(enc_in[t]))
        cot = bf16(f32(cot) + b)
    c0 = bf16(f32(cot) + f32(skip[1]))

    sent = lax.ppermute(jnp.where(lower, c0, a_last), "pipe", [(1, 0), (pipe_size - 2, pipe_size - 1)])
    acts_lo = jnp.stack([a0] + [enc_act[t] for t in range(1, half)])
    cots_lo = jnp.stack([sent] + [enc_c[t] for t in range(1, half)])
    acts_up = jnp.stack([sent] + [dec_act[t] for t in range(1, half)])
    cots_up = jnp.stack([seed] + [dec_c[t] for t in range(1, half)])
    act_sel = jnp.where(lower, acts_lo[stage], acts_up[stage])
    cot_sel = jnp.where(lower, cots_lo[stage], cots_up[stage])
    both = jnp.concatenate([act_sel, cot_sel], axis=-1)
    every = lax.all_gather(both, ("dp", "mp"), axis=0, tiled=True)
    act_all = every[..., :channels]
    cot_all = lax.dynamic_slice_in_dim(every, channels + low, chan_half, 3)
    grad = weight_grad(act_all, cot_all)
    return grad.reshape(1, -1)


def solution(mesh):
    return jax.shard_map(
        local,
        mesh=mesh,
        in_specs=(
            P(("groups", "dp"), None, None, None, None, None),
            P("pipe", None, "mp"),
            P(("groups", "dp"), None, None, None, None, None),
        ),
        out_specs=P(("groups", "pipe"), "mp"),
        check_vma=False,
    )
```

```python
import jax
import jax.numpy as jnp
from jax import lax
from jax.sharding import PartitionSpec as P


def silu_slope(pre_act):
    sigmoid = jax.nn.sigmoid(pre_act)
    return sigmoid * (1.0 + pre_act * (1.0 - sigmoid))


def conv(act, weight):
    return lax.conv_general_dilated(
        act, weight, (1, 1), ((1, 1), (1, 1)),
        dimension_numbers=("NHWC", "OHWI", "NHWC"),
        preferred_element_type=jnp.float32,
    )


def conv_t(cot, weight):
    flipped = jnp.flip(cot, (1, 2))
    out = lax.conv_general_dilated(
        flipped, weight, (1, 1), ((1, 1), (1, 1)),
        dimension_numbers=("NHWC", "IHWO", "NHWC"),
        preferred_element_type=jnp.float32,
    )
    return jnp.flip(out, (1, 2))


def weight_grad(act, cot):
    return lax.conv_general_dilated(
        act, cot, (1, 1), ((1, 1), (1, 1)),
        dimension_numbers=("CHWN", "IHWO", "CHWN"),
        preferred_element_type=jnp.float32,
    )


def f32(v):
    return v.astype(jnp.float32)


def bf16(v):
    return v.astype(jnp.bfloat16)


def local(latent, section_weight, out_grad):
    pipe_size = lax.axis_size("pipe")
    half = pipe_size // 2
    device = lax.axis_index("pipe")
    lower = device < half
    stage = jnp.minimum(device, pipe_size - 1 - device)
    lane = lax.axis_index("mp")
    swap = [(0, 1), (1, 0)]

    channels = latent.shape[-1]
    img = latent.shape[-3:]
    samples = latent.reshape((-1,) + img)
    grads = out_grad.reshape((-1,) + img)
    per_lane = samples.shape[0] // 2
    mine = lane * per_lane
    theirs = (1 - lane) * per_lane

    chan_half = section_weight.shape[-1] // (9 * channels)
    own = lax.optimization_barrier(
        section_weight[0].reshape(2, chan_half, 9, channels).transpose(0, 2, 1, 3)
        .reshape(2, 3, 3, chan_half, channels)
    ).transpose(0, 3, 1, 2, 4)
    other = lax.ppermute(own, "mp", swap)

    def up(t, v):
        pairs = [(t, t + 1), (pipe_size - 1 - t, pipe_size - 2 - t)]
        return lax.ppermute(v, "pipe", pairs)

    def down(t, v):
        pairs = [(t, t - 1), (pipe_size - 1 - t, pipe_size - t)]
        return lax.ppermute(v, "pipe", pairs)

    def take(v, at):
        return lax.dynamic_slice_in_dim(v, at, per_lane, 0)

    def join(first, second):
        return jnp.where(lane == 0, jnp.concatenate([first, second], -1),
                         jnp.concatenate([second, first], -1))

    low = lane * chan_half
    act_all = bf16(jax.nn.silu(f32(samples)))
    own_in = lax.dynamic_slice_in_dim(samples, low, chan_half, 3)
    h1_half = bf16(f32(own_in) + conv(act_all, own[0]))
    seed_half = lax.dynamic_slice_in_dim(grads, low, chan_half, 3)
    d_part = conv_t(seed_half, own[1])
    parts = lax.all_gather(jnp.concatenate([f32(h1_half), d_part], -1), "mp", axis=0, tiled=False)
    h1 = take(bf16(jnp.concatenate([parts[0, ..., :chan_half], parts[1, ..., :chan_half]], -1)), mine)
    d_last = take(parts[0, ..., chan_half:] + parts[1, ..., chan_half:], mine)
    x0 = take(samples, mine)
    a0 = take(act_all, mine)
    seed = take(grads, mine)
    h1_r = up(0, h1)
    d_last_r = up(0, d_last)

    other, _ = lax.optimization_barrier((other, h1))
    full = jnp.where(lane == 0, jnp.concatenate([own, other], 1),
                     jnp.concatenate([other, own], 1))
    w_enc, w_dec = full[0], full[1]

    enc_in, enc_act, enc_out = {}, {}, {}
    enc_in[0], enc_act[0], enc_out[0] = x0, a0, h1
    received = h1_r
    for t in range(1, half):
        h_in = received
        u = f32(h_in)
        a = bf16(jax.nn.silu(u))
        h_out = bf16(u + conv(a, w_enc))
        enc_in[t], enc_act[t], enc_out[t] = h_in, a, h_out
        if t < half - 1:
            received = up(t, h_out)

    dec_u, dec_act, dec_c = {}, {}, {}
    h_in = enc_out[half - 1]
    u = f32(h_in) + f32(h_in)
    a = bf16(jax.nn.silu(u))
    current = bf16(f32(h_in) + conv(a, w_dec))
    dec_u[half - 1], dec_act[half - 1] = u, a
    for t in range(half - 2, 0, -1):
        h_in = down(t + 1, current)
        u = f32(h_in) + f32(enc_out[t])
        a = bf16(jax.nn.silu(u))
        current = bf16(f32(h_in) + conv(a, w_dec))
        dec_u[t], dec_act[t] = u, a

    u_last = f32(current) + f32(h1_r)
    a_last = bf16(jax.nn.silu(u_last))
    b_last = d_last_r * silu_slope(u_last)
    skip = {1: bf16(b_last)}
    cot = bf16(f32(seed) + b_last)

    for t in range(1, half):
        if t > 1:
            cot = up(t - 1, cot)
        dec_c[t] = cot
        d = conv_t(cot, w_dec)
        b = d * silu_slope(dec_u[t])
        g = bf16(f32(cot) + b)
        if t < half - 1:
            skip[t + 1] = bf16(b)
            cot = g
        else:
            cot = bf16(f32(g) + b)

    enc_c = {}
    for t in range(half - 1, 0, -1):
        if t < half - 1:
            cot = bf16(f32(down(t + 1, cot)) + f32(skip[t + 1]))
        enc_c[t] = cot
        d = conv_t(cot, w_enc)
        b = d * silu_slope(f32(enc_in[t]))
        cot = bf16(f32(cot) + b)
    c0 = bf16(f32(cot) + f32(skip[1]))

    sent = lax.ppermute(jnp.where(lower, c0, a_last), "pipe", [(1, 0), (pipe_size - 2, pipe_size - 1)])
    acts_lo = jnp.stack([a0] + [enc_act[t] for t in range(1, half)])
    cots_lo = jnp.stack([sent] + [enc_c[t] for t in range(1, half)])
    acts_up = jnp.stack([sent] + [dec_act[t] for t in range(1, half)])
    cots_up = jnp.stack([seed] + [dec_c[t] for t in range(1, half)])
    act_sel = jnp.where(lower, acts_lo[stage], acts_up[stage])
    cot_sel = jnp.where(lower, cots_lo[stage], cots_up[stage])
    both = jnp.concatenate([act_sel, cot_sel], axis=-1)
    every = lax.all_gather(both, ("mp", "dp"), axis=0, tiled=True)
    act_all = every[..., :channels]
    cot_all = lax.dynamic_slice_in_dim(every, channels + low, chan_half, 3)
    grad = weight_grad(act_all, cot_all)
    return grad.reshape(1, -1)


def solution(mesh):
    return jax.shard_map(
        local,
        mesh=mesh,
        in_specs=(
            P(("groups", "dp"), None, None, None, None, None),
            P("pipe", None, "mp"),
            P(("groups", "dp"), None, None, None, None, None),
        ),
        out_specs=P(("groups", "pipe"), "mp"),
        check_vma=False,
    )
```

```python
import jax
import jax.numpy as jnp
from jax import lax
from jax.sharding import PartitionSpec as P


def silu_slope(pre_act):
    sigmoid = jax.nn.sigmoid(pre_act)
    return sigmoid * (1.0 + pre_act * (1.0 - sigmoid))


def conv(act, weight):
    return lax.conv_general_dilated(
        act, weight, (1, 1), ((1, 1), (1, 1)),
        dimension_numbers=("NHWC", "OHWI", "NHWC"),
        preferred_element_type=jnp.float32,
    )


def conv_t(cot, weight):
    flipped = jnp.flip(cot, (1, 2))
    out = lax.conv_general_dilated(
        flipped, weight, (1, 1), ((1, 1), (1, 1)),
        dimension_numbers=("NHWC", "IHWO", "NHWC"),
        preferred_element_type=jnp.float32,
    )
    return jnp.flip(out, (1, 2))


def weight_grad(act, cot):
    return lax.conv_general_dilated(
        act, cot, (1, 1), ((1, 1), (1, 1)),
        dimension_numbers=("CHWN", "IHWO", "CHWN"),
        preferred_element_type=jnp.float32,
    )


def f32(v):
    return v.astype(jnp.float32)


def bf16(v):
    return v.astype(jnp.bfloat16)


def local(latent, section_weight, out_grad):
    pipe_size = lax.axis_size("pipe")
    half = pipe_size // 2
    device = lax.axis_index("pipe")
    lower = device < half
    stage = jnp.minimum(device, pipe_size - 1 - device)
    lane = lax.axis_index("mp")
    swap = [(0, 1), (1, 0)]

    channels = latent.shape[-1]
    img = latent.shape[-3:]
    samples = latent.reshape((-1,) + img)
    grads = out_grad.reshape((-1,) + img)
    per_lane = samples.shape[0] // 2
    mine = lane * per_lane
    theirs = (1 - lane) * per_lane

    chan_half = section_weight.shape[-1] // (9 * channels)
    own = lax.optimization_barrier(
        section_weight[0].reshape(2, chan_half, 9, channels).transpose(0, 2, 1, 3)
        .reshape(2, 3, 3, chan_half, channels)
    ).transpose(0, 3, 1, 2, 4)
    other = lax.ppermute(own, "mp", swap)

    def up(t, v):
        pairs = [(t, t + 1), (pipe_size - 1 - t, pipe_size - 2 - t)]
        return lax.ppermute(v, "pipe", pairs)

    def down(t, v):
        pairs = [(t, t - 1), (pipe_size - 1 - t, pipe_size - t)]
        return lax.ppermute(v, "pipe", pairs)

    def take(v, at):
        return lax.dynamic_slice_in_dim(v, at, per_lane, 0)

    def join(first, second):
        return jnp.where(lane == 0, jnp.concatenate([first, second], -1),
                         jnp.concatenate([second, first], -1))

    low = lane * chan_half
    high = (1 - lane) * chan_half
    x0 = take(samples, mine)
    seed = take(grads, mine)
    a0 = bf16(jax.nn.silu(f32(x0)))
    h1_own = conv(a0, own[0])
    d_own = conv_t(lax.dynamic_slice_in_dim(seed, low, chan_half, 3), own[1])
    h1 = bf16(f32(x0) + join(h1_own, conv(a0, other[0])))
    d_last = d_own + conv_t(lax.dynamic_slice_in_dim(seed, high, chan_half, 3), other[1])
    h1_r = up(0, h1)
    d_last_r = up(0, d_last)

    other, _ = lax.optimization_barrier((other, h1))
    full = jnp.where(lane == 0, jnp.concatenate([own, other], 1),
                     jnp.concatenate([other, own], 1))
    w_enc, w_dec = full[0], full[1]

    enc_in, enc_act, enc_out = {}, {}, {}
    enc_in[0], enc_act[0], enc_out[0] = x0, a0, h1
    received = h1_r
    for t in range(1, half):
        h_in = received
        u = f32(h_in)
        a = bf16(jax.nn.silu(u))
        h_out = bf16(u + conv(a, w_enc))
        enc_in[t], enc_act[t], enc_out[t] = h_in, a, h_out
        if t < half - 1:
            received = up(t, h_out)

    dec_u, dec_act, dec_c = {}, {}, {}
    h_in = enc_out[half - 1]
    u = f32(h_in) + f32(h_in)
    a = bf16(jax.nn.silu(u))
    current = bf16(f32(h_in) + conv(a, w_dec))
    dec_u[half - 1], dec_act[half - 1] = u, a
    for t in range(half - 2, 0, -1):
        h_in = down(t + 1, current)
        u = f32(h_in) + f32(enc_out[t])
        a = bf16(jax.nn.silu(u))
        current = bf16(f32(h_in) + conv(a, w_dec))
        dec_u[t], dec_act[t] = u, a

    u_last = f32(current) + f32(h1_r)
    a_last = bf16(jax.nn.silu(u_last))
    b_last = d_last_r * silu_slope(u_last)
    skip = {1: bf16(b_last)}
    cot = bf16(f32(seed) + b_last)

    for t in range(1, half):
        if t > 1:
            cot = up(t - 1, cot)
        dec_c[t] = cot
        d = conv_t(cot, w_dec)
        b = d * silu_slope(dec_u[t])
        g = bf16(f32(cot) + b)
        if t < half - 1:
            skip[t + 1] = bf16(b)
            cot = g
        else:
            cot = bf16(f32(g) + b)

    enc_c = {}
    for t in range(half - 1, 0, -1):
        if t < half - 1:
            cot = bf16(f32(down(t + 1, cot)) + f32(skip[t + 1]))
        enc_c[t] = cot
        d = conv_t(cot, w_enc)
        b = d * silu_slope(f32(enc_in[t]))
        cot = bf16(f32(cot) + b)
    c0 = bf16(f32(cot) + f32(skip[1]))

    sent = lax.ppermute(jnp.where(lower, c0, a_last), "pipe", [(1, 0), (pipe_size - 2, pipe_size - 1)])
    acts_lo = jnp.stack([a0] + [enc_act[t] for t in range(1, half)])
    cots_lo = jnp.stack([sent] + [enc_c[t] for t in range(1, half)])
    acts_up = jnp.stack([sent] + [dec_act[t] for t in range(1, half)])
    cots_up = jnp.stack([seed] + [dec_c[t] for t in range(1, half)])
    act_sel = jnp.where(lower, acts_lo[stage], acts_up[stage])
    cot_sel = jnp.where(lower, cots_lo[stage], cots_up[stage])
    both = jnp.concatenate([act_sel, cot_sel], axis=-1)
    every = lax.all_gather(both, ("dp", "mp"), axis=0, tiled=True)
    act_all = every[..., :channels]
    cot_all = lax.dynamic_slice_in_dim(every, channels + low, chan_half, 3)
    grad = weight_grad(act_all, cot_all)
    return grad.reshape(1, -1)


def solution(mesh):
    return jax.shard_map(
        local,
        mesh=mesh,
        in_specs=(
            P(("groups", "dp"), None, None, None, None, None),
            P("pipe", None, "mp"),
            P(("groups", "dp"), None, None, None, None, None),
        ),
        out_specs=P(("groups", "pipe"), "mp"),
        check_vma=False,
    )
```

```python
import jax
import jax.numpy as jnp
from jax import lax
from jax.sharding import PartitionSpec as P


def silu_slope(pre_act):
    sigmoid = jax.nn.sigmoid(pre_act)
    return sigmoid * (1.0 + pre_act * (1.0 - sigmoid))


def conv(act, weight):
    return lax.conv_general_dilated(
        act, weight, (1, 1), ((1, 1), (1, 1)),
        dimension_numbers=("NHWC", "OHWI", "NHWC"),
        preferred_element_type=jnp.float32,
    )


def conv_t(cot, weight):
    flipped = jnp.flip(cot, (1, 2))
    out = lax.conv_general_dilated(
        flipped, weight, (1, 1), ((1, 1), (1, 1)),
        dimension_numbers=("NHWC", "IHWO", "NHWC"),
        preferred_element_type=jnp.float32,
    )
    return jnp.flip(out, (1, 2))


def weight_grad(act, cot):
    return lax.conv_general_dilated(
        act, cot, (1, 1), ((1, 1), (1, 1)),
        dimension_numbers=("CHWN", "IHWO", "CHWN"),
        preferred_element_type=jnp.float32,
    )


def f32(v):
    return v.astype(jnp.float32)


def bf16(v):
    return v.astype(jnp.bfloat16)


def on_stage(active, fn, *args):
    shapes = jax.eval_shape(fn, *args)

    def idle(*unused):
        return jax.tree.map(lambda v: jnp.zeros(v.shape, v.dtype), shapes)

    return lax.cond(active, fn, idle, *args)


def local(latent, section_weight, out_grad):
    pipe_size = lax.axis_size("pipe")
    half = pipe_size // 2
    device = lax.axis_index("pipe")
    lower = device < half
    stage = jnp.minimum(device, pipe_size - 1 - device)
    lane = lax.axis_index("mp")
    swap = [(0, 1), (1, 0)]

    channels = latent.shape[-1]
    img = latent.shape[-3:]
    samples = latent.reshape((-1,) + img)
    grads = out_grad.reshape((-1,) + img)
    per_lane = samples.shape[0] // 2
    mine = lane * per_lane
    theirs = (1 - lane) * per_lane

    chan_half = section_weight.shape[-1] // (9 * channels)
    own = lax.optimization_barrier(
        section_weight[0].reshape(2, chan_half, 9, channels).transpose(0, 2, 1, 3)
        .reshape(2, 3, 3, chan_half, channels)
    ).transpose(0, 3, 1, 2, 4)
    other = lax.ppermute(own, "mp", swap)

    def up(t, v):
        pairs = [(t, t + 1), (pipe_size - 1 - t, pipe_size - 2 - t)]
        return lax.ppermute(v, "pipe", pairs)

    def down(t, v):
        pairs = [(t, t - 1), (pipe_size - 1 - t, pipe_size - t)]
        return lax.ppermute(v, "pipe", pairs)

    def take(v, at):
        return lax.dynamic_slice_in_dim(v, at, per_lane, 0)

    def join(first, second):
        return jnp.where(lane == 0, jnp.concatenate([first, second], -1),
                         jnp.concatenate([second, first], -1))

    low = lane * chan_half
    high = (1 - lane) * chan_half
    x0 = take(samples, mine)
    seed = take(grads, mine)
    a0 = bf16(jax.nn.silu(f32(x0)))

    def first(x0, a0, seed, own, other):
        h1_own = conv(a0, own[0])
        d_own = conv_t(lax.dynamic_slice_in_dim(seed, low, chan_half, 3), own[1])
        h1 = bf16(f32(x0) + join(h1_own, conv(a0, other[0])))
        return h1, d_own + conv_t(lax.dynamic_slice_in_dim(seed, high, chan_half, 3), other[1])

    h1, d_last = on_stage(stage == 0, first, x0, a0, seed, own, other)
    h1_r = up(0, h1)
    d_last_r = up(0, d_last)

    other, _ = lax.optimization_barrier((other, h1))
    full = jnp.where(lane == 0, jnp.concatenate([own, other], 1),
                     jnp.concatenate([other, own], 1))
    w_enc, w_dec = full[0], full[1]

    enc_in, enc_act, enc_out = {}, {}, {}
    enc_in[0], enc_act[0], enc_out[0] = x0, a0, h1
    received = h1_r
    for t in range(1, half):
        h_in = received
        u = f32(h_in)
        a = bf16(jax.nn.silu(u))
        h_out = bf16(u + conv(a, w_enc))
        enc_in[t], enc_act[t], enc_out[t] = h_in, a, h_out
        if t < half - 1:
            received = up(t, h_out)

    dec_u, dec_act, dec_c = {}, {}, {}
    h_in = enc_out[half - 1]
    u = f32(h_in) + f32(h_in)
    a = bf16(jax.nn.silu(u))
    current = bf16(f32(h_in) + conv(a, w_dec))
    dec_u[half - 1], dec_act[half - 1] = u, a
    for t in range(half - 2, 0, -1):
        h_in = down(t + 1, current)
        u = f32(h_in) + f32(enc_out[t])
        a = bf16(jax.nn.silu(u))
        current = bf16(f32(h_in) + conv(a, w_dec))
        dec_u[t], dec_act[t] = u, a

    u_last = f32(current) + f32(h1_r)
    a_last = bf16(jax.nn.silu(u_last))
    b_last = d_last_r * silu_slope(u_last)
    skip = {1: bf16(b_last)}
    cot = bf16(f32(seed) + b_last)

    for t in range(1, half):
        if t > 1:
            cot = up(t - 1, cot)
        dec_c[t] = cot
        d = conv_t(cot, w_dec)
        b = d * silu_slope(dec_u[t])
        g = bf16(f32(cot) + b)
        if t < half - 1:
            skip[t + 1] = bf16(b)
            cot = g
        else:
            cot = bf16(f32(g) + b)

    enc_c = {}
    for t in range(half - 1, 0, -1):
        if t < half - 1:
            cot = bf16(f32(down(t + 1, cot)) + f32(skip[t + 1]))
        enc_c[t] = cot
        d = conv_t(cot, w_enc)
        b = d * silu_slope(f32(enc_in[t]))
        cot = bf16(f32(cot) + b)
    c0 = bf16(f32(cot) + f32(skip[1]))

    sent = lax.ppermute(jnp.where(lower, c0, a_last), "pipe", [(1, 0), (pipe_size - 2, pipe_size - 1)])
    acts_lo = jnp.stack([a0] + [enc_act[t] for t in range(1, half)])
    cots_lo = jnp.stack([sent] + [enc_c[t] for t in range(1, half)])
    acts_up = jnp.stack([sent] + [dec_act[t] for t in range(1, half)])
    cots_up = jnp.stack([seed] + [dec_c[t] for t in range(1, half)])
    act_sel = jnp.where(lower, acts_lo[stage], acts_up[stage])
    cot_sel = jnp.where(lower, cots_lo[stage], cots_up[stage])
    both = jnp.concatenate([act_sel, cot_sel], axis=-1)
    every = lax.all_gather(both, ("dp", "mp"), axis=0, tiled=True)
    act_all = every[..., :channels]
    cot_all = lax.dynamic_slice_in_dim(every, channels + low, chan_half, 3)
    grad = weight_grad(act_all, cot_all)
    return grad.reshape(1, -1)


def solution(mesh):
    return jax.shard_map(
        local,
        mesh=mesh,
        in_specs=(
            P(("groups", "dp"), None, None, None, None, None),
            P("pipe", None, "mp"),
            P(("groups", "dp"), None, None, None, None, None),
        ),
        out_specs=P(("groups", "pipe"), "mp"),
        check_vma=False,
    )
```

```python
import jax
import jax.numpy as jnp
from jax import lax
from jax.sharding import PartitionSpec as P


def silu_slope(pre_act):
    sigmoid = jax.nn.sigmoid(pre_act)
    return sigmoid * (1.0 + pre_act * (1.0 - sigmoid))


def conv(act, weight):
    return lax.conv_general_dilated(
        act, weight, (1, 1), ((1, 1), (1, 1)),
        dimension_numbers=("NHWC", "OHWI", "NHWC"),
        preferred_element_type=jnp.float32,
    )


def conv_t(cot, weight):
    flipped = jnp.flip(cot, (1, 2))
    out = lax.conv_general_dilated(
        flipped, weight, (1, 1), ((1, 1), (1, 1)),
        dimension_numbers=("NHWC", "IHWO", "NHWC"),
        preferred_element_type=jnp.float32,
    )
    return jnp.flip(out, (1, 2))


def weight_grad(act, cot):
    return lax.conv_general_dilated(
        act, cot, (1, 1), ((1, 1), (1, 1)),
        dimension_numbers=("CHWN", "IHWO", "CHWN"),
        preferred_element_type=jnp.float32,
    )


def f32(v):
    return v.astype(jnp.float32)


def bf16(v):
    return v.astype(jnp.bfloat16)


def on_stage(active, fn, *args):
    shapes = jax.eval_shape(fn, *args)

    def idle(*unused):
        return jax.tree.map(lambda v: jnp.zeros(v.shape, v.dtype), shapes)

    return lax.cond(active, fn, idle, *args)


def local(latent, section_weight, out_grad):
    pipe_size = lax.axis_size("pipe")
    half = pipe_size // 2
    device = lax.axis_index("pipe")
    lower = device < half
    stage = jnp.minimum(device, pipe_size - 1 - device)
    lane = lax.axis_index("mp")
    swap = [(0, 1), (1, 0)]

    channels = latent.shape[-1]
    img = latent.shape[-3:]
    samples = latent.reshape((-1,) + img)
    grads = out_grad.reshape((-1,) + img)
    per_lane = samples.shape[0] // 2
    mine = lane * per_lane
    theirs = (1 - lane) * per_lane

    chan_half = section_weight.shape[-1] // (9 * channels)
    own = lax.optimization_barrier(
        section_weight[0].reshape(2, chan_half, 9, channels).transpose(0, 2, 1, 3)
        .reshape(2, 3, 3, chan_half, channels)
    ).transpose(0, 3, 1, 2, 4)
    other = lax.ppermute(own, "mp", swap)

    def up(t, v):
        pairs = [(t, t + 1), (pipe_size - 1 - t, pipe_size - 2 - t)]
        return lax.ppermute(v, "pipe", pairs)

    def down(t, v):
        pairs = [(t, t - 1), (pipe_size - 1 - t, pipe_size - t)]
        return lax.ppermute(v, "pipe", pairs)

    def take(v, at):
        return lax.dynamic_slice_in_dim(v, at, per_lane, 0)

    def join(first, second):
        return jnp.where(lane == 0, jnp.concatenate([first, second], -1),
                         jnp.concatenate([second, first], -1))

    low = lane * chan_half
    high = (1 - lane) * chan_half
    x0 = take(samples, mine)
    seed = take(grads, mine)
    a0 = bf16(jax.nn.silu(f32(x0)))

    def first_own(a0, seed, own):
        return conv(a0, own[0]), conv_t(lax.dynamic_slice_in_dim(seed, low, chan_half, 3), own[1])

    def first_other(x0, a0, seed, other, h1_own, d_own):
        h1 = bf16(f32(x0) + join(h1_own, conv(a0, other[0])))
        return h1, d_own + conv_t(lax.dynamic_slice_in_dim(seed, high, chan_half, 3), other[1])

    h1_own, d_own = on_stage(stage == 0, first_own, a0, seed, own)
    h1, d_last = on_stage(stage == 0, first_other, x0, a0, seed, other, h1_own, d_own)
    h1_r = up(0, h1)
    d_last_r = up(0, d_last)

    other, _ = lax.optimization_barrier((other, h1))
    full = jnp.where(lane == 0, jnp.concatenate([own, other], 1),
                     jnp.concatenate([other, own], 1))
    w_enc, w_dec = full[0], full[1]

    enc_in, enc_act, enc_out = {}, {}, {}
    enc_in[0], enc_act[0], enc_out[0] = x0, a0, h1
    received = h1_r
    for t in range(1, half):
        h_in = received
        u = f32(h_in)
        a = bf16(jax.nn.silu(u))
        h_out = bf16(u + conv(a, w_enc))
        enc_in[t], enc_act[t], enc_out[t] = h_in, a, h_out
        if t < half - 1:
            received = up(t, h_out)

    dec_u, dec_act, dec_c = {}, {}, {}
    h_in = enc_out[half - 1]
    u = f32(h_in) + f32(h_in)
    a = bf16(jax.nn.silu(u))
    current = bf16(f32(h_in) + conv(a, w_dec))
    dec_u[half - 1], dec_act[half - 1] = u, a
    for t in range(half - 2, 0, -1):
        h_in = down(t + 1, current)
        u = f32(h_in) + f32(enc_out[t])
        a = bf16(jax.nn.silu(u))
        current = bf16(f32(h_in) + conv(a, w_dec))
        dec_u[t], dec_act[t] = u, a

    u_last = f32(current) + f32(h1_r)
    a_last = bf16(jax.nn.silu(u_last))
    b_last = d_last_r * silu_slope(u_last)
    skip = {1: bf16(b_last)}
    cot = bf16(f32(seed) + b_last)

    for t in range(1, half):
        if t > 1:
            cot = up(t - 1, cot)
        dec_c[t] = cot
        d = conv_t(cot, w_dec)
        b = d * silu_slope(dec_u[t])
        g = bf16(f32(cot) + b)
        if t < half - 1:
            skip[t + 1] = bf16(b)
            cot = g
        else:
            cot = bf16(f32(g) + b)

    enc_c = {}
    for t in range(half - 1, 0, -1):
        if t < half - 1:
            cot = bf16(f32(down(t + 1, cot)) + f32(skip[t + 1]))
        enc_c[t] = cot
        d = conv_t(cot, w_enc)
        b = d * silu_slope(f32(enc_in[t]))
        cot = bf16(f32(cot) + b)
    c0 = bf16(f32(cot) + f32(skip[1]))

    sent = lax.ppermute(jnp.where(lower, c0, a_last), "pipe", [(1, 0), (pipe_size - 2, pipe_size - 1)])
    acts_lo = jnp.stack([a0] + [enc_act[t] for t in range(1, half)])
    cots_lo = jnp.stack([sent] + [enc_c[t] for t in range(1, half)])
    acts_up = jnp.stack([sent] + [dec_act[t] for t in range(1, half)])
    cots_up = jnp.stack([seed] + [dec_c[t] for t in range(1, half)])
    act_sel = jnp.where(lower, acts_lo[stage], acts_up[stage])
    cot_sel = jnp.where(lower, cots_lo[stage], cots_up[stage])
    both = jnp.concatenate([act_sel, cot_sel], axis=-1)
    every = lax.all_gather(both, ("dp", "mp"), axis=0, tiled=True)
    act_all = every[..., :channels]
    cot_all = lax.dynamic_slice_in_dim(every, channels + low, chan_half, 3)
    grad = weight_grad(act_all, cot_all)
    return grad.reshape(1, -1)


def solution(mesh):
    return jax.shard_map(
        local,
        mesh=mesh,
        in_specs=(
            P(("groups", "dp"), None, None, None, None, None),
            P("pipe", None, "mp"),
            P(("groups", "dp"), None, None, None, None, None),
        ),
        out_specs=P(("groups", "pipe"), "mp"),
        check_vma=False,
    )
```

```python
import jax
import jax.numpy as jnp
from jax import lax
from jax.sharding import PartitionSpec as P


def silu_slope(pre_act):
    sigmoid = jax.nn.sigmoid(pre_act)
    return sigmoid * (1.0 + pre_act * (1.0 - sigmoid))


def conv(act, weight):
    return lax.conv_general_dilated(
        act, weight, (1, 1), ((1, 1), (1, 1)),
        dimension_numbers=("NHWC", "OHWI", "NHWC"),
        preferred_element_type=jnp.float32,
    )


def conv_t(cot, weight):
    flipped = jnp.flip(cot, (1, 2))
    out = lax.conv_general_dilated(
        flipped, weight, (1, 1), ((1, 1), (1, 1)),
        dimension_numbers=("NHWC", "IHWO", "NHWC"),
        preferred_element_type=jnp.float32,
    )
    return jnp.flip(out, (1, 2))


def weight_grad(act, cot):
    return lax.conv_general_dilated(
        act, cot, (1, 1), ((1, 1), (1, 1)),
        dimension_numbers=("CHWN", "IHWO", "CHWN"),
        preferred_element_type=jnp.float32,
    )


def f32(v):
    return v.astype(jnp.float32)


def bf16(v):
    return v.astype(jnp.bfloat16)


def on_stage(active, fn, *args):
    shapes = jax.eval_shape(fn, *args)

    def idle(*unused):
        return jax.tree.map(lambda v: jnp.zeros(v.shape, v.dtype), shapes)

    return lax.cond(active, fn, idle, *args)


def local(latent, section_weight, out_grad):
    pipe_size = lax.axis_size("pipe")
    half = pipe_size // 2
    device = lax.axis_index("pipe")
    lower = device < half
    stage = jnp.minimum(device, pipe_size - 1 - device)
    lane = lax.axis_index("mp")
    swap = [(0, 1), (1, 0)]

    channels = latent.shape[-1]
    img = latent.shape[-3:]
    samples = latent.reshape((-1,) + img)
    grads = out_grad.reshape((-1,) + img)
    per_lane = samples.shape[0] // 2
    mine = lane * per_lane
    theirs = (1 - lane) * per_lane

    chan_half = section_weight.shape[-1] // (9 * channels)
    own = lax.optimization_barrier(
        section_weight[0].reshape(2, chan_half, 9, channels).transpose(0, 2, 1, 3)
        .reshape(2, 3, 3, chan_half, channels)
    ).transpose(0, 3, 1, 2, 4)
    other = lax.ppermute(own, "mp", swap)

    def up(t, v):
        pairs = [(t, t + 1), (pipe_size - 1 - t, pipe_size - 2 - t)]
        return lax.ppermute(v, "pipe", pairs)

    def down(t, v):
        pairs = [(t, t - 1), (pipe_size - 1 - t, pipe_size - t)]
        return lax.ppermute(v, "pipe", pairs)

    def take(v, at):
        return lax.dynamic_slice_in_dim(v, at, per_lane, 0)

    def join(first, second):
        return jnp.where(lane == 0, jnp.concatenate([first, second], -1),
                         jnp.concatenate([second, first], -1))

    low = lane * chan_half
    high = (1 - lane) * chan_half
    x0 = take(samples, mine)
    seed = take(grads, mine)
    a0 = bf16(jax.nn.silu(f32(x0)))

    def first_own(a0, seed, own):
        return conv(a0, own[0]), conv_t(lax.dynamic_slice_in_dim(seed, low, chan_half, 3), own[1])

    def first_h1(x0, a0, other_enc, h1_own):
        return bf16(f32(x0) + join(h1_own, conv(a0, other_enc)))

    def first_d(seed, other_dec, d_own):
        return d_own + conv_t(lax.dynamic_slice_in_dim(seed, high, chan_half, 3), other_dec)

    h1_own, d_own = on_stage(stage == 0, first_own, a0, seed, own)
    h1 = on_stage(stage == 0, first_h1, x0, a0, other[0], h1_own)
    h1_r = up(0, h1)
    d_last = on_stage(stage == 0, first_d, seed, other[1], d_own)
    d_last_r = up(0, d_last)

    other, _ = lax.optimization_barrier((other, h1))
    full = jnp.where(lane == 0, jnp.concatenate([own, other], 1),
                     jnp.concatenate([other, own], 1))
    w_enc, w_dec = full[0], full[1]

    enc_in, enc_act, enc_out = {}, {}, {}
    enc_in[0], enc_act[0], enc_out[0] = x0, a0, h1
    received = h1_r
    for t in range(1, half):
        h_in = received
        u = f32(h_in)
        a = bf16(jax.nn.silu(u))
        h_out = bf16(u + conv(a, w_enc))
        enc_in[t], enc_act[t], enc_out[t] = h_in, a, h_out
        if t < half - 1:
            received = up(t, h_out)

    dec_u, dec_act, dec_c = {}, {}, {}
    h_in = enc_out[half - 1]
    u = f32(h_in) + f32(h_in)
    a = bf16(jax.nn.silu(u))
    current = bf16(f32(h_in) + conv(a, w_dec))
    dec_u[half - 1], dec_act[half - 1] = u, a
    for t in range(half - 2, 0, -1):
        h_in = down(t + 1, current)
        u = f32(h_in) + f32(enc_out[t])
        a = bf16(jax.nn.silu(u))
        current = bf16(f32(h_in) + conv(a, w_dec))
        dec_u[t], dec_act[t] = u, a

    u_last = f32(current) + f32(h1_r)
    a_last = bf16(jax.nn.silu(u_last))
    b_last = d_last_r * silu_slope(u_last)
    skip = {1: bf16(b_last)}
    cot = bf16(f32(seed) + b_last)

    for t in range(1, half):
        if t > 1:
            cot = up(t - 1, cot)
        dec_c[t] = cot
        d = conv_t(cot, w_dec)
        b = d * silu_slope(dec_u[t])
        g = bf16(f32(cot) + b)
        if t < half - 1:
            skip[t + 1] = bf16(b)
            cot = g
        else:
            cot = bf16(f32(g) + b)

    enc_c = {}
    for t in range(half - 1, 0, -1):
        if t < half - 1:
            cot = bf16(f32(down(t + 1, cot)) + f32(skip[t + 1]))
        enc_c[t] = cot
        d = conv_t(cot, w_enc)
        b = d * silu_slope(f32(enc_in[t]))
        cot = bf16(f32(cot) + b)
    c0 = bf16(f32(cot) + f32(skip[1]))

    sent = lax.ppermute(jnp.where(lower, c0, a_last), "pipe", [(1, 0), (pipe_size - 2, pipe_size - 1)])
    acts_lo = jnp.stack([a0] + [enc_act[t] for t in range(1, half)])
    cots_lo = jnp.stack([sent] + [enc_c[t] for t in range(1, half)])
    acts_up = jnp.stack([sent] + [dec_act[t] for t in range(1, half)])
    cots_up = jnp.stack([seed] + [dec_c[t] for t in range(1, half)])
    act_sel = jnp.where(lower, acts_lo[stage], acts_up[stage])
    cot_sel = jnp.where(lower, cots_lo[stage], cots_up[stage])
    both = jnp.concatenate([act_sel, cot_sel], axis=-1)
    every = lax.all_gather(both, ("dp", "mp"), axis=0, tiled=True)
    act_all = every[..., :channels]
    cot_all = lax.dynamic_slice_in_dim(every, channels + low, chan_half, 3)
    grad = weight_grad(act_all, cot_all)
    return grad.reshape(1, -1)


def solution(mesh):
    return jax.shard_map(
        local,
        mesh=mesh,
        in_specs=(
            P(("groups", "dp"), None, None, None, None, None),
            P("pipe", None, "mp"),
            P(("groups", "dp"), None, None, None, None, None),
        ),
        out_specs=P(("groups", "pipe"), "mp"),
        check_vma=False,
    )
```

```python
import jax
import jax.numpy as jnp
from jax import lax
from jax.sharding import PartitionSpec as P


def silu_slope(pre_act):
    sigmoid = jax.nn.sigmoid(pre_act)
    return sigmoid * (1.0 + pre_act * (1.0 - sigmoid))


def conv(act, weight):
    return lax.conv_general_dilated(
        act, weight, (1, 1), ((1, 1), (1, 1)),
        dimension_numbers=("NHWC", "OHWI", "NHWC"),
        preferred_element_type=jnp.float32,
    )


def conv_t(cot, weight):
    flipped = jnp.flip(cot, (1, 2))
    out = lax.conv_general_dilated(
        flipped, weight, (1, 1), ((1, 1), (1, 1)),
        dimension_numbers=("NHWC", "IHWO", "NHWC"),
        preferred_element_type=jnp.float32,
    )
    return jnp.flip(out, (1, 2))


def weight_grad(act, cot):
    return lax.conv_general_dilated(
        act, cot, (1, 1), ((1, 1), (1, 1)),
        dimension_numbers=("CHWN", "IHWO", "CHWN"),
        preferred_element_type=jnp.float32,
    )


def f32(v):
    return v.astype(jnp.float32)


def bf16(v):
    return v.astype(jnp.bfloat16)


def on_stage(active, fn, *args):
    shapes = jax.eval_shape(fn, *args)

    def idle(*unused):
        return jax.tree.map(lambda v: jnp.zeros(v.shape, v.dtype), shapes)

    return lax.cond(active, fn, idle, *args)


def local(latent, section_weight, out_grad):
    pipe_size = lax.axis_size("pipe")
    half = pipe_size // 2
    device = lax.axis_index("pipe")
    lower = device < half
    stage = jnp.minimum(device, pipe_size - 1 - device)
    lane = lax.axis_index("mp")
    swap = [(0, 1), (1, 0)]

    channels = latent.shape[-1]
    img = latent.shape[-3:]
    samples = latent.reshape((-1,) + img)
    grads = out_grad.reshape((-1,) + img)
    per_lane = samples.shape[0] // 2
    mine = lane * per_lane
    theirs = (1 - lane) * per_lane

    chan_half = section_weight.shape[-1] // (9 * channels)
    own = lax.optimization_barrier(
        section_weight[0].reshape(2, chan_half, 9, channels).transpose(0, 2, 1, 3)
        .reshape(2, 3, 3, chan_half, channels)
    ).transpose(0, 3, 1, 2, 4)
    other = lax.ppermute(own, "mp", swap)

    def up(t, v):
        pairs = [(t, t + 1), (pipe_size - 1 - t, pipe_size - 2 - t)]
        return lax.ppermute(v, "pipe", pairs)

    def down(t, v):
        pairs = [(t, t - 1), (pipe_size - 1 - t, pipe_size - t)]
        return lax.ppermute(v, "pipe", pairs)

    def take(v, at):
        return lax.dynamic_slice_in_dim(v, at, per_lane, 0)

    def join(first, second):
        return jnp.where(lane == 0, jnp.concatenate([first, second], -1),
                         jnp.concatenate([second, first], -1))

    low = lane * chan_half
    x0 = take(samples, mine)
    seed = take(grads, mine)
    a0 = bf16(jax.nn.silu(f32(x0)))

    def first(samples, grads, own):
        act_all = bf16(jax.nn.silu(f32(samples)))
        own_in = lax.dynamic_slice_in_dim(samples, low, chan_half, 3)
        h1_half = bf16(f32(own_in) + conv(act_all, own[0]))
        d_part = conv_t(lax.dynamic_slice_in_dim(grads, low, chan_half, 3), own[1])
        return h1_half, d_part

    h1_half, d_part = on_stage(stage == 0, first, samples, grads, own)
    straight = [(0, 1), (pipe_size - 1, pipe_size - 2)]
    across = [(src * 2 + m, dst * 2 + 1 - m) for src, dst in straight for m in range(2)]
    h1_s, d_s = lax.ppermute((take(h1_half, mine), take(d_part, mine)), "pipe", straight)
    h1_c, d_c = lax.ppermute((take(h1_half, theirs), take(d_part, theirs)), ("pipe", "mp"), across)
    h1_r = join(h1_s, h1_c)
    d_last_r = d_s + d_c
    h1 = h1_r

    other, _ = lax.optimization_barrier((other, h1_half))
    full = jnp.where(lane == 0, jnp.concatenate([own, other], 1),
                     jnp.concatenate([other, own], 1))
    w_enc, w_dec = full[0], full[1]

    enc_in, enc_act, enc_out = {}, {}, {}
    enc_in[0], enc_act[0], enc_out[0] = x0, a0, h1
    received = h1_r
    for t in range(1, half):
        h_in = received
        u = f32(h_in)
        a = bf16(jax.nn.silu(u))
        h_out = bf16(u + conv(a, w_enc))
        enc_in[t], enc_act[t], enc_out[t] = h_in, a, h_out
        if t < half - 1:
            received = up(t, h_out)

    dec_u, dec_act, dec_c = {}, {}, {}
    h_in = enc_out[half - 1]
    u = f32(h_in) + f32(h_in)
    a = bf16(jax.nn.silu(u))
    current = bf16(f32(h_in) + conv(a, w_dec))
    dec_u[half - 1], dec_act[half - 1] = u, a
    for t in range(half - 2, 0, -1):
        h_in = down(t + 1, current)
        u = f32(h_in) + f32(enc_out[t])
        a = bf16(jax.nn.silu(u))
        current = bf16(f32(h_in) + conv(a, w_dec))
        dec_u[t], dec_act[t] = u, a

    u_last = f32(current) + f32(h1_r)
    a_last = bf16(jax.nn.silu(u_last))
    b_last = d_last_r * silu_slope(u_last)
    skip = {1: bf16(b_last)}
    cot = bf16(f32(seed) + b_last)

    for t in range(1, half):
        if t > 1:
            cot = up(t - 1, cot)
        dec_c[t] = cot
        d = conv_t(cot, w_dec)
        b = d * silu_slope(dec_u[t])
        g = bf16(f32(cot) + b)
        if t < half - 1:
            skip[t + 1] = bf16(b)
            cot = g
        else:
            cot = bf16(f32(g) + b)

    enc_c = {}
    for t in range(half - 1, 0, -1):
        if t < half - 1:
            cot = bf16(f32(down(t + 1, cot)) + f32(skip[t + 1]))
        enc_c[t] = cot
        d = conv_t(cot, w_enc)
        b = d * silu_slope(f32(enc_in[t]))
        cot = bf16(f32(cot) + b)
    c0 = bf16(f32(cot) + f32(skip[1]))

    sent = lax.ppermute(jnp.where(lower, c0, a_last), "pipe", [(1, 0), (pipe_size - 2, pipe_size - 1)])
    acts_lo = jnp.stack([a0] + [enc_act[t] for t in range(1, half)])
    cots_lo = jnp.stack([sent] + [enc_c[t] for t in range(1, half)])
    acts_up = jnp.stack([sent] + [dec_act[t] for t in range(1, half)])
    cots_up = jnp.stack([seed] + [dec_c[t] for t in range(1, half)])
    act_sel = jnp.where(lower, acts_lo[stage], acts_up[stage])
    cot_sel = jnp.where(lower, cots_lo[stage], cots_up[stage])
    both = jnp.concatenate([act_sel, cot_sel], axis=-1)
    every = lax.all_gather(both, ("dp", "mp"), axis=0, tiled=True)
    act_all = every[..., :channels]
    cot_all = lax.dynamic_slice_in_dim(every, channels + low, chan_half, 3)
    grad = weight_grad(act_all, cot_all)
    return grad.reshape(1, -1)


def solution(mesh):
    return jax.shard_map(
        local,
        mesh=mesh,
        in_specs=(
            P(("groups", "dp"), None, None, None, None, None),
            P("pipe", None, "mp"),
            P(("groups", "dp"), None, None, None, None, None),
        ),
        out_specs=P(("groups", "pipe"), "mp"),
        check_vma=False,
    )
```

```python
import jax
import jax.numpy as jnp
from jax import lax
from jax.sharding import PartitionSpec as P


def silu_slope(pre_act):
    sigmoid = jax.nn.sigmoid(pre_act)
    return sigmoid * (1.0 + pre_act * (1.0 - sigmoid))


def conv(act, weight):
    return lax.conv_general_dilated(
        act, weight, (1, 1), ((1, 1), (1, 1)),
        dimension_numbers=("NHWC", "OHWI", "NHWC"),
        preferred_element_type=jnp.float32,
    )


def conv_t(cot, weight):
    flipped = jnp.flip(cot, (1, 2))
    out = lax.conv_general_dilated(
        flipped, weight, (1, 1), ((1, 1), (1, 1)),
        dimension_numbers=("NHWC", "IHWO", "NHWC"),
        preferred_element_type=jnp.float32,
    )
    return jnp.flip(out, (1, 2))


def conv_flipped(flipped, weight):
    return lax.conv_general_dilated(
        flipped, weight, (1, 1), ((1, 1), (1, 1)),
        dimension_numbers=("NHWC", "IHWO", "NHWC"),
        preferred_element_type=jnp.float32,
    )


def weight_grad(act, cot):
    return lax.conv_general_dilated(
        act, cot, (1, 1), ((1, 1), (1, 1)),
        dimension_numbers=("CHWN", "IHWO", "CHWN"),
        preferred_element_type=jnp.float32,
    )


def f32(v):
    return v.astype(jnp.float32)


def bf16(v):
    return v.astype(jnp.bfloat16)


def on_stage(active, fn, *args):
    shapes = jax.eval_shape(fn, *args)

    def idle(*unused):
        return jax.tree.map(lambda v: jnp.zeros(v.shape, v.dtype), shapes)

    return lax.cond(active, fn, idle, *args)


def local(latent, section_weight, out_grad):
    pipe_size = lax.axis_size("pipe")
    half = pipe_size // 2
    device = lax.axis_index("pipe")
    lower = device < half
    stage = jnp.minimum(device, pipe_size - 1 - device)
    lane = lax.axis_index("mp")
    swap = [(0, 1), (1, 0)]

    channels = latent.shape[-1]
    img = latent.shape[-3:]
    samples = latent.reshape((-1,) + img)
    grads = out_grad.reshape((-1,) + img)
    per_lane = samples.shape[0] // 2
    mine = lane * per_lane
    theirs = (1 - lane) * per_lane

    chan_half = section_weight.shape[-1] // (9 * channels)
    own = lax.optimization_barrier(
        section_weight[0].reshape(2, chan_half, 9, channels).transpose(0, 2, 1, 3)
        .reshape(2, 3, 3, chan_half, channels)
    ).transpose(0, 3, 1, 2, 4)
    other = lax.ppermute(own, "mp", swap)

    def up(t, v):
        pairs = [(t, t + 1), (pipe_size - 1 - t, pipe_size - 2 - t)]
        return lax.ppermute(v, "pipe", pairs)

    def down(t, v):
        pairs = [(t, t - 1), (pipe_size - 1 - t, pipe_size - t)]
        return lax.ppermute(v, "pipe", pairs)

    def take(v, at):
        return lax.dynamic_slice_in_dim(v, at, per_lane, 0)

    def join(first, second):
        return jnp.where(lane == 0, jnp.concatenate([first, second], -1),
                         jnp.concatenate([second, first], -1))

    low = lane * chan_half
    high = (1 - lane) * chan_half
    x0 = take(samples, mine)
    seed = take(grads, mine)
    a0 = bf16(jax.nn.silu(f32(x0)))

    def first_own(a0, seed, own):
        flipped = jnp.flip(seed, (1, 2))
        d_own = conv_flipped(lax.dynamic_slice_in_dim(flipped, low, chan_half, 3), own[1])
        return conv(a0, own[0]), d_own

    def first_h1(x0, a0, other_enc, h1_own):
        return bf16(f32(x0) + join(h1_own, conv(a0, other_enc)))

    def first_d(seed, other_dec, d_own):
        flipped = jnp.flip(seed, (1, 2))
        d_other = conv_flipped(lax.dynamic_slice_in_dim(flipped, high, chan_half, 3), other_dec)
        return jnp.flip(d_own + d_other, (1, 2))

    h1_own, d_own = on_stage(stage == 0, first_own, a0, seed, own)
    h1 = on_stage(stage == 0, first_h1, x0, a0, other[0], h1_own)
    h1_r = up(0, h1)
    d_last = on_stage(stage == 0, first_d, seed, other[1], d_own)
    d_last_r = up(0, d_last)

    other, _ = lax.optimization_barrier((other, h1))
    full = jnp.where(lane == 0, jnp.concatenate([own, other], 1),
                     jnp.concatenate([other, own], 1))
    w_enc, w_dec = full[0], full[1]

    enc_in, enc_act, enc_out = {}, {}, {}
    enc_in[0], enc_act[0], enc_out[0] = x0, a0, h1
    received = h1_r
    for t in range(1, half):
        h_in = received
        u = f32(h_in)
        a = bf16(jax.nn.silu(u))
        h_out = bf16(u + conv(a, w_enc))
        enc_in[t], enc_act[t], enc_out[t] = h_in, a, h_out
        if t < half - 1:
            received = up(t, h_out)

    dec_u, dec_act, dec_c = {}, {}, {}
    h_in = enc_out[half - 1]
    u = f32(h_in) + f32(h_in)
    a = bf16(jax.nn.silu(u))
    current = bf16(f32(h_in) + conv(a, w_dec))
    dec_u[half - 1], dec_act[half - 1] = u, a
    for t in range(half - 2, 0, -1):
        h_in = down(t + 1, current)
        u = f32(h_in) + f32(enc_out[t])
        a = bf16(jax.nn.silu(u))
        current = bf16(f32(h_in) + conv(a, w_dec))
        dec_u[t], dec_act[t] = u, a

    u_last = f32(current) + f32(h1_r)
    a_last = bf16(jax.nn.silu(u_last))
    b_last = d_last_r * silu_slope(u_last)
    skip = {1: bf16(b_last)}
    cot = bf16(f32(seed) + b_last)

    for t in range(1, half):
        if t > 1:
            cot = up(t - 1, cot)
        dec_c[t] = cot
        d = conv_t(cot, w_dec)
        b = d * silu_slope(dec_u[t])
        g = bf16(f32(cot) + b)
        if t < half - 1:
            skip[t + 1] = bf16(b)
            cot = g
        else:
            cot = bf16(f32(g) + b)

    enc_c = {}
    for t in range(half - 1, 0, -1):
        if t < half - 1:
            cot = bf16(f32(down(t + 1, cot)) + f32(skip[t + 1]))
        enc_c[t] = cot
        d = conv_t(cot, w_enc)
        b = d * silu_slope(f32(enc_in[t]))
        cot = bf16(f32(cot) + b)
    c0 = bf16(f32(cot) + f32(skip[1]))

    sent = lax.ppermute(jnp.where(lower, c0, a_last), "pipe", [(1, 0), (pipe_size - 2, pipe_size - 1)])
    acts_lo = jnp.stack([a0] + [enc_act[t] for t in range(1, half)])
    cots_lo = jnp.stack([sent] + [enc_c[t] for t in range(1, half)])
    acts_up = jnp.stack([sent] + [dec_act[t] for t in range(1, half)])
    cots_up = jnp.stack([seed] + [dec_c[t] for t in range(1, half)])
    act_sel = jnp.where(lower, acts_lo[stage], acts_up[stage])
    cot_sel = jnp.where(lower, cots_lo[stage], cots_up[stage])
    both = jnp.concatenate([act_sel, cot_sel], axis=-1)
    every = lax.all_gather(both, ("dp", "mp"), axis=0, tiled=True)
    act_all = every[..., :channels]
    cot_all = lax.dynamic_slice_in_dim(every, channels + low, chan_half, 3)
    grad = weight_grad(act_all, cot_all)
    return grad.reshape(1, -1)


def solution(mesh):
    return jax.shard_map(
        local,
        mesh=mesh,
        in_specs=(
            P(("groups", "dp"), None, None, None, None, None),
            P("pipe", None, "mp"),
            P(("groups", "dp"), None, None, None, None, None),
        ),
        out_specs=P(("groups", "pipe"), "mp"),
        check_vma=False,
    )
```

```python
import jax
import jax.numpy as jnp
from jax import lax
from jax.sharding import PartitionSpec as P


def silu_slope(pre_act):
    sigmoid = jax.nn.sigmoid(pre_act)
    return sigmoid * (1.0 + pre_act * (1.0 - sigmoid))


def conv(act, weight):
    return lax.conv_general_dilated(
        act, weight, (1, 1), ((1, 1), (1, 1)),
        dimension_numbers=("NHWC", "OHWI", "NHWC"),
        preferred_element_type=jnp.float32,
    )


def conv_t(cot, weight):
    flipped = jnp.flip(cot, (1, 2))
    out = lax.conv_general_dilated(
        flipped, weight, (1, 1), ((1, 1), (1, 1)),
        dimension_numbers=("NHWC", "IHWO", "NHWC"),
        preferred_element_type=jnp.float32,
    )
    return jnp.flip(out, (1, 2))


def conv_flipped(flipped, weight):
    return lax.conv_general_dilated(
        flipped, weight, (1, 1), ((1, 1), (1, 1)),
        dimension_numbers=("NHWC", "IHWO", "NHWC"),
        preferred_element_type=jnp.float32,
    )


def weight_grad(act, cot):
    return lax.conv_general_dilated(
        act, cot, (1, 1), ((1, 1), (1, 1)),
        dimension_numbers=("CHWN", "IHWO", "CHWN"),
        preferred_element_type=jnp.float32,
    )


def f32(v):
    return v.astype(jnp.float32)


def bf16(v):
    return v.astype(jnp.bfloat16)


def on_stage(active, fn, *args):
    shapes = jax.eval_shape(fn, *args)

    def idle(*unused):
        return jax.tree.map(lambda v: jnp.zeros(v.shape, v.dtype), shapes)

    return lax.cond(active, fn, idle, *args)


def local(latent, section_weight, out_grad):
    pipe_size = lax.axis_size("pipe")
    half = pipe_size // 2
    device = lax.axis_index("pipe")
    lower = device < half
    stage = jnp.minimum(device, pipe_size - 1 - device)
    lane = lax.axis_index("mp")
    swap = [(0, 1), (1, 0)]

    channels = latent.shape[-1]
    img = latent.shape[-3:]
    samples = latent.reshape((-1,) + img)
    grads = out_grad.reshape((-1,) + img)
    per_lane = samples.shape[0] // 2
    mine = lane * per_lane
    theirs = (1 - lane) * per_lane

    chan_half = section_weight.shape[-1] // (9 * channels)
    own = lax.optimization_barrier(
        section_weight[0].reshape(2, chan_half, 9, channels).transpose(0, 2, 1, 3)
        .reshape(2, 3, 3, chan_half, channels)
    ).transpose(0, 3, 1, 2, 4)
    other = lax.ppermute(own, "mp", swap)

    def up(t, v):
        pairs = [(t, t + 1), (pipe_size - 1 - t, pipe_size - 2 - t)]
        return lax.ppermute(v, "pipe", pairs)

    def down(t, v):
        pairs = [(t, t - 1), (pipe_size - 1 - t, pipe_size - t)]
        return lax.ppermute(v, "pipe", pairs)

    def take(v, at):
        return lax.dynamic_slice_in_dim(v, at, per_lane, 0)

    def join(first, second):
        return jnp.where(lane == 0, jnp.concatenate([first, second], -1),
                         jnp.concatenate([second, first], -1))

    low = lane * chan_half
    high = (1 - lane) * chan_half
    x0 = take(samples, mine)
    seed = take(grads, mine)
    a0 = bf16(jax.nn.silu(f32(x0)))

    def first_own(a0, seed, own):
        flipped = jnp.flip(seed, (1, 2))
        d_own = conv_flipped(lax.dynamic_slice_in_dim(flipped, low, chan_half, 3), own[1])
        return conv(a0, own[0]), d_own

    def first_h1(x0, a0, other_enc, h1_own):
        return bf16(f32(x0) + join(h1_own, conv(a0, other_enc)))

    def first_d(seed, other_dec, d_own):
        flipped = jnp.flip(seed, (1, 2))
        d_other = conv_flipped(lax.dynamic_slice_in_dim(flipped, high, chan_half, 3), other_dec)
        return jnp.flip(d_own + d_other, (1, 2))

    h1_own, d_own = on_stage(stage == 0, first_own, a0, seed, own)
    h1 = on_stage(stage == 0, first_h1, x0, a0, other[0], h1_own)
    h1_r = up(0, h1)
    d_last = on_stage(stage == 0, first_d, seed, other[1], d_own)
    d_last_r = up(0, d_last)

    other, _ = lax.optimization_barrier((other, h1))
    full = jnp.where(lane == 0, jnp.concatenate([own, other], 1),
                     jnp.concatenate([other, own], 1))
    w_enc, w_dec = full[0], full[1]

    enc_in, enc_act, enc_out = {}, {}, {}
    enc_in[0], enc_act[0], enc_out[0] = x0, a0, h1
    received = h1_r
    for t in range(1, half):
        h_in = received
        u = f32(h_in)
        a = bf16(jax.nn.silu(u))
        h_out = bf16(u + conv(a, w_enc))
        enc_in[t], enc_act[t], enc_out[t] = h_in, a, h_out
        if t < half - 1:
            received = up(t, h_out)

    dec_u, dec_act, dec_c = {}, {}, {}
    h_in = enc_out[half - 1]
    u = f32(h_in) + f32(h_in)
    a = bf16(jax.nn.silu(u))
    current = bf16(f32(h_in) + conv(a, w_dec))
    dec_u[half - 1], dec_act[half - 1] = u, a
    for t in range(half - 2, 0, -1):
        h_in = down(t + 1, current)
        u = f32(h_in) + f32(enc_out[t])
        a = bf16(jax.nn.silu(u))
        current = bf16(f32(h_in) + conv(a, w_dec))
        dec_u[t], dec_act[t] = u, a

    u_last = f32(current) + f32(h1_r)
    a_last = bf16(jax.nn.silu(u_last))
    b_last = d_last_r * silu_slope(u_last)
    def flip(v):
        return jnp.flip(v, (1, 2))

    skip_f = {1: flip(bf16(b_last))}
    cot = bf16(f32(seed) + b_last)
    cot_f = flip(cot)

    for t in range(1, half):
        if t > 1:
            cot = up(t - 1, cot)
            cot_f = flip(cot)
        dec_c[t] = cot
        b_f = conv_flipped(cot_f, w_dec) * flip(silu_slope(dec_u[t]))
        g_f = bf16(f32(cot_f) + b_f)
        if t < half - 1:
            skip_f[t + 1] = bf16(b_f)
            cot = flip(g_f)
        else:
            cot_f = bf16(f32(g_f) + b_f)

    enc_c = {}
    for t in range(half - 1, 0, -1):
        if t < half - 1:
            cot_f = bf16(f32(flip(down(t + 1, flip(cot_f)))) + f32(skip_f[t + 1]))
        enc_c[t] = flip(cot_f)
        b_f = conv_flipped(cot_f, w_enc) * flip(silu_slope(f32(enc_in[t])))
        cot_f = bf16(f32(cot_f) + b_f)
    c0 = flip(bf16(f32(cot_f) + f32(skip_f[1])))

    sent = lax.ppermute(jnp.where(lower, c0, a_last), "pipe", [(1, 0), (pipe_size - 2, pipe_size - 1)])
    acts_lo = jnp.stack([a0] + [enc_act[t] for t in range(1, half)])
    cots_lo = jnp.stack([sent] + [enc_c[t] for t in range(1, half)])
    acts_up = jnp.stack([sent] + [dec_act[t] for t in range(1, half)])
    cots_up = jnp.stack([seed] + [dec_c[t] for t in range(1, half)])
    act_sel = jnp.where(lower, acts_lo[stage], acts_up[stage])
    cot_sel = jnp.where(lower, cots_lo[stage], cots_up[stage])
    both = jnp.concatenate([act_sel, cot_sel], axis=-1)
    every = lax.all_gather(both, ("dp", "mp"), axis=0, tiled=True)
    act_all = every[..., :channels]
    cot_all = lax.dynamic_slice_in_dim(every, channels + low, chan_half, 3)
    grad = weight_grad(act_all, cot_all)
    return grad.reshape(1, -1)


def solution(mesh):
    return jax.shard_map(
        local,
        mesh=mesh,
        in_specs=(
            P(("groups", "dp"), None, None, None, None, None),
            P("pipe", None, "mp"),
            P(("groups", "dp"), None, None, None, None, None),
        ),
        out_specs=P(("groups", "pipe"), "mp"),
        check_vma=False,
    )
```

```python
import jax
import jax.numpy as jnp
from jax import lax
from jax.sharding import PartitionSpec as P


def silu_slope(pre_act):
    sigmoid = jax.nn.sigmoid(pre_act)
    return sigmoid * (1.0 + pre_act * (1.0 - sigmoid))


def conv(act, weight):
    return lax.conv_general_dilated(
        act, weight, (1, 1), ((1, 1), (1, 1)),
        dimension_numbers=("NHWC", "OHWI", "NHWC"),
        preferred_element_type=jnp.float32,
    )


def conv_t(cot, weight):
    flipped = jnp.flip(cot, (1, 2))
    out = lax.conv_general_dilated(
        flipped, weight, (1, 1), ((1, 1), (1, 1)),
        dimension_numbers=("NHWC", "IHWO", "NHWC"),
        preferred_element_type=jnp.float32,
    )
    return jnp.flip(out, (1, 2))


def conv_flipped(flipped, weight):
    return lax.conv_general_dilated(
        flipped, weight, (1, 1), ((1, 1), (1, 1)),
        dimension_numbers=("NHWC", "IHWO", "NHWC"),
        preferred_element_type=jnp.float32,
    )


def weight_grad(act, cot):
    return lax.conv_general_dilated(
        act, cot, (1, 1), ((1, 1), (1, 1)),
        dimension_numbers=("CHWN", "IHWO", "CHWN"),
        preferred_element_type=jnp.float32,
    )


def f32(v):
    return v.astype(jnp.float32)


def bf16(v):
    return v.astype(jnp.bfloat16)


def on_stage(active, fn, *args):
    shapes = jax.eval_shape(fn, *args)

    def idle(*unused):
        return jax.tree.map(lambda v: jnp.zeros(v.shape, v.dtype), shapes)

    return lax.cond(active, fn, idle, *args)


def local(latent, section_weight, out_grad):
    pipe_size = lax.axis_size("pipe")
    half = pipe_size // 2
    device = lax.axis_index("pipe")
    lower = device < half
    stage = jnp.minimum(device, pipe_size - 1 - device)
    lane = lax.axis_index("mp")
    swap = [(0, 1), (1, 0)]

    channels = latent.shape[-1]
    img = latent.shape[-3:]
    samples = latent.reshape((-1,) + img)
    grads = out_grad.reshape((-1,) + img)
    per_lane = samples.shape[0] // 2
    mine = lane * per_lane
    theirs = (1 - lane) * per_lane

    chan_half = section_weight.shape[-1] // (9 * channels)
    own = lax.optimization_barrier(
        section_weight[0].reshape(2, chan_half, 9, channels).transpose(0, 2, 1, 3)
        .reshape(2, 3, 3, chan_half, channels)
    ).transpose(0, 3, 1, 2, 4)
    other = lax.ppermute(own, "mp", swap)

    def up(t, v):
        pairs = [(t, t + 1), (pipe_size - 1 - t, pipe_size - 2 - t)]
        return lax.ppermute(v, "pipe", pairs)

    def down(t, v):
        pairs = [(t, t - 1), (pipe_size - 1 - t, pipe_size - t)]
        return lax.ppermute(v, "pipe", pairs)

    def take(v, at):
        return lax.dynamic_slice_in_dim(v, at, per_lane, 0)

    def join(first, second):
        return jnp.where(lane == 0, jnp.concatenate([first, second], -1),
                         jnp.concatenate([second, first], -1))

    low = lane * chan_half
    high = (1 - lane) * chan_half
    x0 = take(samples, mine)
    seed = take(grads, mine)
    a0 = bf16(jax.nn.silu(f32(x0)))

    def first_own(a0, seed, own):
        flipped = jnp.flip(seed, (1, 2))
        d_own = conv_flipped(lax.dynamic_slice_in_dim(flipped, low, chan_half, 3), own[1])
        return conv(a0, own[0]), d_own

    def first_h1(x0, a0, other_enc, h1_own):
        return bf16(f32(x0) + join(h1_own, conv(a0, other_enc)))

    def first_d(seed, other_dec, d_own):
        flipped = jnp.flip(seed, (1, 2))
        d_other = conv_flipped(lax.dynamic_slice_in_dim(flipped, high, chan_half, 3), other_dec)
        return jnp.flip(d_own + d_other, (1, 2))

    h1_own, d_own = first_own(a0, seed, own)
    h1 = on_stage(stage == 0, first_h1, x0, a0, other[0], h1_own)
    h1_r = up(0, h1)
    d_last = on_stage(stage == 0, first_d, seed, other[1], d_own)
    d_last_r = up(0, d_last)

    other, _ = lax.optimization_barrier((other, h1))
    full = jnp.where(lane == 0, jnp.concatenate([own, other], 1),
                     jnp.concatenate([other, own], 1))
    w_enc, w_dec = full[0], full[1]

    enc_in, enc_act, enc_out = {}, {}, {}
    enc_in[0], enc_act[0], enc_out[0] = x0, a0, h1
    received = h1_r
    for t in range(1, half):
        h_in = received
        u = f32(h_in)
        a = bf16(jax.nn.silu(u))
        h_out = bf16(u + conv(a, w_enc))
        enc_in[t], enc_act[t], enc_out[t] = h_in, a, h_out
        if t < half - 1:
            received = up(t, h_out)

    dec_u, dec_act, dec_c = {}, {}, {}
    h_in = enc_out[half - 1]
    u = f32(h_in) + f32(h_in)
    a = bf16(jax.nn.silu(u))
    current = bf16(f32(h_in) + conv(a, w_dec))
    dec_u[half - 1], dec_act[half - 1] = u, a
    for t in range(half - 2, 0, -1):
        h_in = down(t + 1, current)
        u = f32(h_in) + f32(enc_out[t])
        a = bf16(jax.nn.silu(u))
        current = bf16(f32(h_in) + conv(a, w_dec))
        dec_u[t], dec_act[t] = u, a

    u_last = f32(current) + f32(h1_r)
    a_last = bf16(jax.nn.silu(u_last))
    b_last = d_last_r * silu_slope(u_last)
    skip = {1: bf16(b_last)}
    cot = bf16(f32(seed) + b_last)

    for t in range(1, half):
        if t > 1:
            cot = up(t - 1, cot)
        dec_c[t] = cot
        d = conv_t(cot, w_dec)
        b = d * silu_slope(dec_u[t])
        g = bf16(f32(cot) + b)
        if t < half - 1:
            skip[t + 1] = bf16(b)
            cot = g
        else:
            cot = bf16(f32(g) + b)

    enc_c = {}
    for t in range(half - 1, 0, -1):
        if t < half - 1:
            cot = bf16(f32(down(t + 1, cot)) + f32(skip[t + 1]))
        enc_c[t] = cot
        d = conv_t(cot, w_enc)
        b = d * silu_slope(f32(enc_in[t]))
        cot = bf16(f32(cot) + b)
    c0 = bf16(f32(cot) + f32(skip[1]))

    sent = lax.ppermute(jnp.where(lower, c0, a_last), "pipe", [(1, 0), (pipe_size - 2, pipe_size - 1)])
    acts_lo = jnp.stack([a0] + [enc_act[t] for t in range(1, half)])
    cots_lo = jnp.stack([sent] + [enc_c[t] for t in range(1, half)])
    acts_up = jnp.stack([sent] + [dec_act[t] for t in range(1, half)])
    cots_up = jnp.stack([seed] + [dec_c[t] for t in range(1, half)])
    act_sel = jnp.where(lower, acts_lo[stage], acts_up[stage])
    cot_sel = jnp.where(lower, cots_lo[stage], cots_up[stage])
    both = jnp.concatenate([act_sel, cot_sel], axis=-1)
    every = lax.all_gather(both, ("dp", "mp"), axis=0, tiled=True)
    act_all = every[..., :channels]
    cot_all = lax.dynamic_slice_in_dim(every, channels + low, chan_half, 3)
    grad = weight_grad(act_all, cot_all)
    return grad.reshape(1, -1)


def solution(mesh):
    return jax.shard_map(
        local,
        mesh=mesh,
        in_specs=(
            P(("groups", "dp"), None, None, None, None, None),
            P("pipe", None, "mp"),
            P(("groups", "dp"), None, None, None, None, None),
        ),
        out_specs=P(("groups", "pipe"), "mp"),
        check_vma=False,
    )
```
